128 devices in a mesh: req: 4 (over z), wide: 32 (over x, y, core).
Axes of the slice: x: 4, y: 4, z: 4, core: 2. Of those that a mesh axis runs over, the one named last changes fastest.
Arguments:
- tokens: bfloat16 [512, 7168], P(('req', 'wide')), may hold values from -6 to 6
- attn_gain: bfloat16 [7168], replicated, may hold values from 0.099609375 to 1.8984375
- qkv_weight: bfloat16 [7168, 3, 7168], P(None, None, 'wide'), may hold values from -0.122756126 to 0.122756126
- adapter_down: bfloat16 [7168, 384], P('wide'), may hold values from -0.0625 to 0.0625
- adapter_up: bfloat16 [3, 128, 7168], P(None, None, 'wide'), may hold values from -0.5 to 0.5
- out_weight: bfloat16 [7168, 3584], P('wide'), may hold values from -0.0625 to 0.0625
- mlp_gain: bfloat16 [3584], replicated, may hold values from 0.099609375 to 1.8984375
- gate_up: bfloat16 [2, 14336, 3584], P(None, ('req', 'wide')), may hold values from -0.09375 to 0.09375
- down_weight: bfloat16 [14336, 3584], P(('req', 'wide')), may hold values from -0.046875 to 0.046875
- key_cache: bfloat16 [4, 8192, 7168], P('req', 'wide'), may hold values from -12 to 12
- value_cache: bfloat16 [4, 8192, 7168], P('req', 'wide'), may hold values from -6 to 6
- cache_lengths: int32 [4], P('req'), may hold values from 129 to 8192, as said below
- slot_mask: int32 [4, 8192], P('req', 'wide'), may hold values 0 or 1
- span_counts: int32 [4], P('req'), may hold values from 32 to 128, as said below
Outputs:
- hidden_out: bfloat16 [512, 3584], P(('req', 'wide'))
- attention: bfloat16 [512, 7168], P('req', 'wide')
- new_keys: bfloat16 [512, 7168], P('req', 'wide')
- new_values: bfloat16 [512, 7168], P('req', 'wide')
The draws below stay inside these ranges and needn't reach their ends.
Inputs may be any that keep to these rules, and one draw needn't show every extreme that they name: `cache_lengths`: the longest request has exactly 8192 filled positions in every draw. `span_counts`: some request fills all 128 slots in every draw.
All inputs are finite; a program needn't handle non-finite values. No bound on the sum of `slot_mask` on one device may be relied on, other than what follows from the above.
Results may differ from the reference program's by a relative error of at most 0.024.
Values may be sent and summed in bfloat16 or wider, within the bound.
No kernel may reach another device: no remote copies, remote signals or barrier semaphores. Data moves between devices by JAX's collectives and lax.ppermute only.
A program may use at most 512 MiB of HBM per device.

```python
import jax
import jax.numpy as jnp
from jax import lax

D = 7168
HID = 3584
HEADS = 32
HD = 224
RANK = 128
FF = 14336
SPAN = 128
REQS = 4
CAP = 8192
TOKENS = 512


def request_lengths(key):
    first_key, second_key, third_key = jax.random.split(jax.random.fold_in(key, 3), 3)
    shifts = jax.random.randint(first_key, (REQS,), 0, 6)
    ceiling = jnp.right_shift(jnp.full((REQS,), CAP, jnp.int32), shifts.astype(jnp.int32))
    reduction = jax.random.randint(second_key, (REQS,), 0, ceiling // 2)
    lengths = ceiling - reduction
    longest = jax.random.randint(third_key, (), 0, REQS)
    return jnp.where(jnp.arange(REQS) == longest, CAP, lengths).astype(jnp.int32)


def draw_cache_lengths(key, part):
    return request_lengths(key)


def draw_span_counts(key, part):
    first_key, second_key = jax.random.split(jax.random.fold_in(key, 7), 2)
    counts = jax.random.randint(first_key, (REQS,), SPAN // 4, SPAN + 1)
    fullest = jax.random.randint(second_key, (), 0, REQS)
    return jnp.where(jnp.arange(REQS) == fullest, SPAN, counts).astype(jnp.int32)


def draw_tokens(key, part):
    noise_key = jax.random.fold_in(jax.random.fold_in(key, 17), 0)
    values = jax.random.normal(noise_key, (TOKENS, D), jnp.float32)
    return jnp.clip(values, -6.0, 6.0).astype(jnp.bfloat16)


def draw_qkv_weight(key, part):
    sigma = (D // 3) ** (-0.5)
    values = sigma * jax.random.normal(jax.random.fold_in(key, 19), (D, 3, D), jnp.float32)
    return jnp.clip(values, -6.0 * sigma, 6.0 * sigma).astype(jnp.bfloat16)


def draw_key_cache(key, part):
    values = 2.0 * jax.random.normal(jax.random.fold_in(key, 23), (REQS, CAP, D), jnp.float32)
    values = jnp.clip(values, -12.0, 12.0)
    return values.astype(jnp.bfloat16)


def touch_ends(values, own_key, low, top_value):
    dims = values.shape
    place = [jax.random.randint(jax.random.fold_in(own_key, axis), (), 0, dims[axis]) for axis in range(len(dims))]
    values = values.at[tuple(place)].set(low)
    longest = dims.index(max(dims))
    place[longest] = (place[longest] + 1) % dims[longest]
    return values.at[tuple(place)].set(top_value)


def level_of(stream_key, shape, pieces, smallest, top_value):
    def one(axis_at, parts):
        steps = jax.random.uniform(jax.random.fold_in(jax.random.fold_in(stream_key, 6), axis_at), (parts,), jnp.float32, smallest / len(pieces), top_value / len(pieces))
        return jnp.repeat(jnp.exp(steps), shape[axis_at] // parts).reshape((-1,) + (1,) * (len(shape) - axis_at - 1))

    factor_of = one(*pieces[0])
    for cut in pieces[1:]:
        factor_of = factor_of * one(*cut)
    return factor_of


def bell_draw(own_key, extent, spread, reach, cuts=(), held_as=jnp.bfloat16):
    array = spread * jax.random.normal(own_key, extent, jnp.float32)
    if cuts:
        array = array * level_of(own_key, extent, cuts, -0.22, 0.18)
    return jnp.clip(array, -reach, reach).astype(held_as)


def setup_inputs(seed: int = 0) -> dict:
    splits = jax.random.split(jax.random.key(seed), 15)
    tokens = draw_tokens(jax.random.fold_in(splits[14], 71), 0)
    attn_gain = jnp.clip(1.0 + 0.18 * jax.random.normal(splits[1], (D,), jnp.float32), 0.099609375, 1.8984375).astype(jnp.bfloat16)
    qkv_weight = draw_qkv_weight(jax.random.fold_in(splits[14], 71), 0)
    adapter_down = bell_draw(splits[3], (D, 3 * RANK), D ** -0.5, 0.0625, ((0, 32),))
    adapter_up = bell_draw(splits[4], (3, RANK, D), RANK ** -0.5, 0.5, ((2, 32),))
    out_weight = bell_draw(splits[5], (D, HID), D ** -0.5, 0.0625, ((0, 32),))
    mlp_gain = jnp.clip(1.0 + 0.18 * jax.random.normal(splits[6], (HID,), jnp.float32), 0.099609375, 1.8984375).astype(jnp.bfloat16)
    gate_up = bell_draw(splits[7], (2, FF, HID), HID ** -0.5, 0.09375, ((1, 128),))
    down_weight = bell_draw(splits[8], (FF, HID), FF ** -0.5, 0.046875, ((0, 128),))
    key_cache = draw_key_cache(jax.random.fold_in(splits[14], 71), 0)
    value_cache = bell_draw(splits[10], (REQS, CAP, D), 1.0, 6.0, ((0, 4), (1, 32)))
    cache_lengths = draw_cache_lengths(jax.random.fold_in(splits[14], 71), 0)
    slot_mask = touch_ends((jax.random.randint(splits[12], (REQS, CAP), 0, 8) < 7).astype(jnp.int32), jax.random.fold_in(splits[12], 1), 0, 1)
    span_counts = draw_span_counts(jax.random.fold_in(splits[14], 71), 0)
    return dict(tokens=tokens, attn_gain=attn_gain, qkv_weight=qkv_weight, adapter_down=adapter_down, adapter_up=adapter_up, out_weight=out_weight, mlp_gain=mlp_gain, gate_up=gate_up, down_weight=down_weight, key_cache=key_cache, value_cache=value_cache, cache_lengths=cache_lengths, slot_mask=slot_mask, span_counts=span_counts)


EPSILON = 1e-05
NEG_LARGE = -1e+30

def rms_scale(values, gains):
    widened = values.astype(jnp.float32)
    meansq = lax.optimization_barrier(jnp.mean(widened * widened, axis=-1, keepdims=True))
    return (widened * lax.rsqrt(meansq + EPSILON) * gains.astype(jnp.float32)).astype(jnp.bfloat16)

def attend(inputs):
    query_rows, keys_old, values_old, keys_new, values_new, length, filled, span_count = inputs
    score_scale = HD ** (-0.5)
    query_heads = query_rows.reshape(SPAN, HEADS, HD).astype(jnp.float32)
    all_keys = jnp.concatenate([keys_old, keys_new], 0).reshape(CAP + SPAN, HEADS, HD).astype(jnp.float32)
    all_values = jnp.concatenate([values_old, values_new], 0).reshape(CAP + SPAN, HEADS, HD).astype(jnp.float32)
    scores = jnp.einsum('qhd,khd->hqk', query_heads, all_keys) * score_scale
    positions = jnp.arange(CAP)
    cache_ok = (positions < length) & (filled == 1)
    query_pos = jnp.arange(SPAN)[:, None]
    key_pos = jnp.arange(SPAN)[None, :]
    span_ok = (key_pos <= query_pos) & ((key_pos < span_count) | (key_pos == query_pos))
    allowed = jnp.concatenate([jnp.broadcast_to(cache_ok[None, :], (SPAN, CAP)), span_ok], 1)
    scores = jnp.where(allowed[None], scores, NEG_LARGE)
    highest = lax.optimization_barrier(jnp.max(scores, axis=-1, keepdims=True))
    weights = jnp.where(allowed[None], jnp.exp(scores - highest), 0.0)
    totals = lax.optimization_barrier(jnp.sum(weights, axis=-1))
    rounded = weights.astype(jnp.bfloat16).astype(jnp.float32)
    mixed = jnp.einsum('hqk,khd->qhd', rounded, all_values)
    result = mixed / jnp.transpose(totals)[:, :, None]
    return result.reshape(SPAN, D).astype(jnp.bfloat16)

def reference(tokens, attn_gain, qkv_weight, adapter_down, adapter_up, out_weight, mlp_gain, gate_up, down_weight, key_cache, value_cache, cache_lengths, slot_mask, span_counts):
    normed = rms_scale(tokens, attn_gain)
    base_part = jnp.dot(normed, qkv_weight.reshape(D, 3 * D), preferred_element_type=jnp.float32).reshape(TOKENS, 3, D)
    lowrank = jnp.dot(normed, adapter_down, preferred_element_type=jnp.float32).astype(jnp.bfloat16)
    adapted = jnp.einsum('tcr,crd->tcd', lowrank.reshape(TOKENS, 3, RANK).astype(jnp.float32), adapter_up.astype(jnp.float32))
    projected = (base_part + adapted).astype(jnp.bfloat16)
    query_all = projected[:, 0]
    new_keys = projected[:, 1]
    new_values = projected[:, 2]
    attention = lax.map(attend, (query_all.reshape(REQS, SPAN, D), key_cache, value_cache, new_keys.reshape(REQS, SPAN, D), new_values.reshape(REQS, SPAN, D), cache_lengths, slot_mask, span_counts))
    attention = attention.reshape(TOKENS, D)
    attn_out = jnp.dot(attention, out_weight, preferred_element_type=jnp.float32)
    normed_mid = rms_scale(attn_out, mlp_gain)
    both = jnp.einsum('td,cfd->ctf', normed_mid.astype(jnp.float32), gate_up.astype(jnp.float32))
    hidden = (jax.nn.silu(both[0]) * both[1]).astype(jnp.bfloat16)
    mlp_out = jnp.dot(hidden, down_weight, preferred_element_type=jnp.float32)
    hidden_out = mlp_out.astype(jnp.bfloat16)
    return (hidden_out, attention, new_keys, new_values)
```

```python
import jax
import jax.numpy as jnp
from jax import lax
from jax.sharding import PartitionSpec as P

D = 7168
HEADS = 32
HD = 224
RANK = 128
SPAN = 128


EPSILON = 1e-05
NEG_LARGE = -1e30
ALL = ("req", "wide")


def rms_scale(values, gains):
    widened = values.astype(jnp.float32)
    meansq = jnp.mean(widened * widened, axis=-1, keepdims=True)
    return (widened * lax.rsqrt(meansq + EPSILON) * gains.astype(jnp.float32)).astype(jnp.bfloat16)


def gather_rows(piece, axis, count):
    flat = piece.reshape(1, -1)
    spread = jnp.broadcast_to(flat, (count, flat.shape[1]))
    return lax.all_to_all(spread, axis, 0, 0, tiled=True)


def send_rows(values, axis, count):
    return lax.all_to_all(values.reshape(count, -1), axis, 0, 0, tiled=True)


def split_pair(values):
    high = lax.reduce_precision(values, exponent_bits=8, mantissa_bits=7)
    low = lax.reduce_precision(values - high, exponent_bits=8, mantissa_bits=7)
    return high, low


def join_pair(high, low):
    return high.astype(jnp.float32) + low.astype(jnp.float32)


def body(
    tokens,
    attn_gain,
    qkv_weight,
    adapter_down,
    adapter_up,
    out_weight,
    mlp_gain,
    gate_up,
    down_weight,
    key_cache,
    value_cache,
    cache_lengths,
    slot_mask,
    span_counts,
):
    score_scale = HD ** (-0.5)
    wide_size = lax.psum(1, "wide")
    all_size = lax.psum(1, ALL)
    local_width = qkv_weight.shape[2]
    local_heads = local_width // HD
    own_rows = tokens.shape[0]
    wide_index = lax.axis_index("wide")
    feature_start = wide_index * local_width

    normed = rms_scale(tokens, attn_gain)
    shard_rows = gather_rows(normed, "wide", wide_size).reshape(SPAN, D)
    base_part = jnp.dot(
        shard_rows, qkv_weight.reshape(D, 3 * local_width), preferred_element_type=jnp.float32
    )
    sliced = lax.dynamic_slice_in_dim(shard_rows, feature_start, local_width, 1)
    partial_low = jnp.dot(sliced, adapter_down, preferred_element_type=jnp.float32)
    low_parts = send_rows(partial_low, "wide", wide_size)
    own_low = jnp.sum(low_parts, axis=0).astype(jnp.bfloat16).reshape(own_rows, 3 * RANK)
    lowrank = gather_rows(own_low, "wide", wide_size).reshape(SPAN, 3, RANK)
    adapted = jnp.einsum("tcr,crd->tcd", lowrank, adapter_up, preferred_element_type=jnp.float32)
    projected = (base_part.reshape(SPAN, 3, local_width) + adapted).astype(jnp.bfloat16)
    query_own = projected[:, 0]
    new_keys = projected[:, 1]
    new_values = projected[:, 2]

    query_heads = gather_rows(query_own, "wide", wide_size).reshape(HEADS, SPAN, HD)
    block_len = key_cache.shape[1]
    block_start = wide_index * block_len
    length = cache_lengths[0]
    usable = (block_start + jnp.arange(block_len) < length) & (slot_mask[0] == 1)

    def cache_block(unused):
        key_heads = key_cache[0].reshape(block_len, HEADS, HD)
        value_heads = value_cache[0].reshape(block_len, HEADS, HD)
        scores = (
            jnp.einsum("hqd,khd->hqk", query_heads, key_heads, preferred_element_type=jnp.float32)
            * score_scale
        )
        scores = jnp.where(usable, scores, NEG_LARGE)
        highest = jnp.max(scores, axis=-1)
        high, low = split_pair(highest)
        reference_max = high + low
        weights = jnp.where(usable, jnp.exp(scores - reference_max[..., None]), 0.0)
        totals = jnp.sum(weights, axis=-1)
        numerator = jnp.einsum(
            "hqk,khd->hqd",
            weights.astype(jnp.bfloat16),
            value_heads,
            preferred_element_type=jnp.float32,
        )
        total_high, total_low = split_pair(totals)
        stats = jnp.stack([high, low, total_high, total_low], axis=-1).astype(jnp.bfloat16)
        return jnp.concatenate([numerator.astype(jnp.bfloat16), stats], axis=-1)

    def skipped(unused):
        stats = jnp.zeros((HEADS, SPAN, 4), jnp.bfloat16).at[..., 0].set(NEG_LARGE)
        return jnp.concatenate([jnp.zeros((HEADS, SPAN, HD), jnp.bfloat16), stats], axis=-1)

    packed = lax.cond(block_start < length, cache_block, skipped, 0)
    parts = lax.all_to_all(packed, "wide", 0, 0, tiled=True)
    part_num = parts[..., :HD].astype(jnp.float32)
    part_max = join_pair(parts[..., HD], parts[..., HD + 1])
    part_sum = join_pair(parts[..., HD + 2], parts[..., HD + 3])

    span_count = span_counts[0]
    query_pos = jnp.arange(SPAN)[:, None]
    key_pos = jnp.arange(SPAN)[None, :]
    span_ok = ((key_pos <= query_pos) & ((key_pos < span_count) | (key_pos == query_pos)))[
        :, None, :
    ]
    own_query = query_own.reshape(SPAN, local_heads, HD)
    own_keys = new_keys.reshape(SPAN, local_heads, HD)
    own_values = new_values.reshape(SPAN, local_heads, HD)
    own_scores = (
        jnp.einsum("qhd,khd->qhk", own_query, own_keys, preferred_element_type=jnp.float32)
        * score_scale
    )
    own_scores = jnp.where(span_ok, own_scores, NEG_LARGE)
    own_max = jnp.max(own_scores, axis=-1)
    own_weights = jnp.where(span_ok, jnp.exp(own_scores - own_max[..., None]), 0.0)
    own_sum = jnp.sum(own_weights, axis=-1)
    own_num = jnp.einsum(
        "qhk,khd->qhd",
        own_weights.astype(jnp.bfloat16),
        own_values,
        preferred_element_type=jnp.float32,
    )
    own_num = own_num.reshape(SPAN, HD)
    own_max = own_max.reshape(SPAN)
    own_sum = own_sum.reshape(SPAN)

    highest = jnp.maximum(jnp.max(part_max, axis=0), own_max)
    part_factor = jnp.exp(part_max - highest)
    own_factor = jnp.exp(own_max - highest)
    numerator = jnp.sum(part_num * part_factor[..., None], axis=0) + own_num * own_factor[:, None]
    totals = jnp.sum(part_sum * part_factor, axis=0) + own_sum * own_factor
    attention = (numerator / totals[:, None]).astype(jnp.bfloat16)

    head_out = jnp.dot(attention, out_weight, preferred_element_type=jnp.float32)
    out_parts = send_rows(head_out.astype(jnp.bfloat16), "wide", wide_size)
    attn_out = jnp.sum(out_parts.astype(jnp.float32), axis=0).reshape(own_rows, -1)
    normed_mid = rms_scale(attn_out, mlp_gain)
    every_row = gather_rows(normed_mid, ALL, all_size).reshape(all_size * own_rows, -1)
    both = jnp.einsum("td,cfd->ctf", every_row, gate_up, preferred_element_type=jnp.float32)
    hidden = (jax.nn.silu(both[0]) * both[1]).astype(jnp.bfloat16)
    ffn_part = jnp.dot(hidden, down_weight, preferred_element_type=jnp.float32)
    ffn_parts = send_rows(ffn_part.astype(jnp.bfloat16), ALL, all_size)
    hidden_out = jnp.sum(ffn_parts.astype(jnp.float32), axis=0).astype(jnp.bfloat16)
    hidden_out = hidden_out.reshape(own_rows, -1)
    return (hidden_out, attention, new_keys, new_values)


def solution(mesh):
    return jax.shard_map(
        body,
        mesh=mesh,
        in_specs=(
            P(("req", "wide"), None),
            P(),
            P(None, None, "wide"),
            P("wide", None),
            P(None, None, "wide"),
            P("wide", None),
            P(),
            P(None, ("req", "wide"), None),
            P(("req", "wide"), None),
            P("req", "wide", None),
            P("req", "wide", None),
            P("req"),
            P("req", "wide"),
            P("req"),
        ),
        out_specs=(P(("req", "wide"), None), P("req", "wide"), P("req", "wide"), P("req", "wide")),
        check_vma=False,
    )
```

```python
import jax
import jax.numpy as jnp
from jax import lax
from jax.sharding import PartitionSpec as P

D = 7168
HEADS = 32
HD = 224
RANK = 128
SPAN = 128


EPSILON = 1e-05
NEG_LARGE = -1e30
ALL = ("req", "wide")


def rms_scale(values, gains):
    widened = values.astype(jnp.float32)
    meansq = jnp.mean(widened * widened, axis=-1, keepdims=True)
    return (widened * lax.rsqrt(meansq + EPSILON) * gains.astype(jnp.float32)).astype(jnp.bfloat16)


def gather_rows(piece, axis, count):
    spread = jnp.broadcast_to(piece[None], (count,) + piece.shape)
    return lax.all_to_all(spread, axis, 0, 0, tiled=True)


def send_rows(values, axis, count):
    blocks = values.reshape((count, values.shape[0] // count) + values.shape[1:])
    return lax.all_to_all(blocks, axis, 0, 0, tiled=True)


def split_pair(values):
    high = lax.reduce_precision(values, exponent_bits=8, mantissa_bits=7)
    low = lax.reduce_precision(values - high, exponent_bits=8, mantissa_bits=7)
    return high, low


def join_pair(high, low):
    return high.astype(jnp.float32) + low.astype(jnp.float32)


def body(
    tokens,
    attn_gain,
    qkv_weight,
    adapter_down,
    adapter_up,
    out_weight,
    mlp_gain,
    gate_up,
    down_weight,
    key_cache,
    value_cache,
    cache_lengths,
    slot_mask,
    span_counts,
):
    score_scale = HD ** (-0.5)
    wide_size = lax.psum(1, "wide")
    all_size = lax.psum(1, ALL)
    local_width = qkv_weight.shape[2]
    local_heads = local_width // HD
    own_rows = tokens.shape[0]
    wide_index = lax.axis_index("wide")
    feature_start = wide_index * local_width

    normed = rms_scale(tokens, attn_gain)
    shard_rows = gather_rows(normed, "wide", wide_size).reshape(SPAN, D)
    base_part = jnp.dot(
        shard_rows, qkv_weight.reshape(D, 3 * local_width), preferred_element_type=jnp.float32
    )
    sliced = lax.dynamic_slice_in_dim(shard_rows, feature_start, local_width, 1)
    partial_low = jnp.dot(sliced, adapter_down, preferred_element_type=jnp.float32)
    low_parts = send_rows(partial_low, "wide", wide_size)
    own_low = jnp.sum(low_parts, axis=0).astype(jnp.bfloat16)
    lowrank = gather_rows(own_low, "wide", wide_size).reshape(SPAN, 3, RANK)
    adapted = jnp.einsum("tcr,crd->tcd", lowrank, adapter_up, preferred_element_type=jnp.float32)
    projected = (base_part.reshape(SPAN, 3, local_width) + adapted).astype(jnp.bfloat16)
    query_own = projected[:, 0]
    new_keys = projected[:, 1]
    new_values = projected[:, 2]

    query_heads = gather_rows(query_own, "wide", wide_size).reshape(HEADS, SPAN, HD)
    block_len = key_cache.shape[1]
    block_start = wide_index * block_len
    length = cache_lengths[0]
    usable = (block_start + jnp.arange(block_len) < length) & (slot_mask[0] == 1)

    def cache_block(unused):
        key_heads = key_cache[0].reshape(block_len, HEADS, HD)
        value_heads = value_cache[0].reshape(block_len, HEADS, HD)
        scores = (
            jnp.einsum("hqd,khd->hqk", query_heads, key_heads, preferred_element_type=jnp.float32)
            * score_scale
        )
        scores = jnp.where(usable, scores, NEG_LARGE)
        highest = jnp.max(scores, axis=-1)
        high, low = split_pair(highest)
        reference_max = high + low
        weights = jnp.where(usable, jnp.exp(scores - reference_max[..., None]), 0.0)
        totals = jnp.sum(weights, axis=-1)
        numerator = jnp.einsum(
            "hqk,khd->hqd",
            weights.astype(jnp.bfloat16),
            value_heads,
            preferred_element_type=jnp.float32,
        )
        total_high, total_low = split_pair(totals)
        stats = jnp.stack([high, low, total_high, total_low], axis=-1).astype(jnp.bfloat16)
        return jnp.concatenate([numerator.astype(jnp.bfloat16), stats], axis=-1)

    def skipped(unused):
        stats = jnp.zeros((HEADS, SPAN, 4), jnp.bfloat16).at[..., 0].set(NEG_LARGE)
        return jnp.concatenate([jnp.zeros((HEADS, SPAN, HD), jnp.bfloat16), stats], axis=-1)

    packed = lax.cond(block_start < length, cache_block, skipped, 0)
    parts = lax.all_to_all(packed, "wide", 0, 0, tiled=True)
    part_num = parts[..., :HD].astype(jnp.float32)
    part_max = join_pair(parts[..., HD], parts[..., HD + 1])
    part_sum = join_pair(parts[..., HD + 2], parts[..., HD + 3])

    span_count = span_counts[0]
    query_pos = jnp.arange(SPAN)[:, None]
    key_pos = jnp.arange(SPAN)[None, :]
    span_ok = ((key_pos <= query_pos) & ((key_pos < span_count) | (key_pos == query_pos)))[
        :, None, :
    ]
    own_query = query_own.reshape(SPAN, local_heads, HD)
    own_keys = new_keys.reshape(SPAN, local_heads, HD)
    own_values = new_values.reshape(SPAN, local_heads, HD)
    own_scores = (
        jnp.einsum("qhd,khd->qhk", own_query, own_keys, preferred_element_type=jnp.float32)
        * score_scale
    )
    own_scores = jnp.where(span_ok, own_scores, NEG_LARGE)
    own_max = jnp.max(own_scores, axis=-1)
    own_weights = jnp.where(span_ok, jnp.exp(own_scores - own_max[..., None]), 0.0)
    own_sum = jnp.sum(own_weights, axis=-1)
    own_num = jnp.einsum(
        "qhk,khd->qhd",
        own_weights.astype(jnp.bfloat16),
        own_values,
        preferred_element_type=jnp.float32,
    )
    own_num = own_num.reshape(SPAN, HD)
    own_max = own_max.reshape(SPAN)
    own_sum = own_sum.reshape(SPAN)

    highest = jnp.maximum(jnp.max(part_max, axis=0), own_max)
    part_factor = jnp.exp(part_max - highest)
    own_factor = jnp.exp(own_max - highest)
    numerator = jnp.sum(part_num * part_factor[..., None], axis=0) + own_num * own_factor[:, None]
    totals = jnp.sum(part_sum * part_factor, axis=0) + own_sum * own_factor
    attention = (numerator / totals[:, None]).astype(jnp.bfloat16)

    head_out = jnp.dot(attention, out_weight, preferred_element_type=jnp.float32)
    out_parts = send_rows(head_out.astype(jnp.bfloat16), "wide", wide_size)
    attn_out = jnp.sum(out_parts.astype(jnp.float32), axis=0)
    normed_mid = rms_scale(attn_out, mlp_gain)
    every_row = gather_rows(normed_mid, ALL, all_size).reshape(all_size * own_rows, -1)
    both = jnp.einsum("td,cfd->ctf", every_row, gate_up, preferred_element_type=jnp.float32)
    hidden = (jax.nn.silu(both[0]) * both[1]).astype(jnp.bfloat16)
    ffn_part = jnp.dot(hidden, down_weight, preferred_element_type=jnp.float32)
    ffn_parts = send_rows(ffn_part.astype(jnp.bfloat16), ALL, all_size)
    hidden_out = jnp.sum(ffn_parts.astype(jnp.float32), axis=0).astype(jnp.bfloat16)
    return (hidden_out, attention, new_keys, new_values)


def solution(mesh):
    return jax.shard_map(
        body,
        mesh=mesh,
        in_specs=(
            P(("req", "wide"), None),
            P(),
            P(None, None, "wide"),
            P("wide", None),
            P(None, None, "wide"),
            P("wide", None),
            P(),
            P(None, ("req", "wide"), None),
            P(("req", "wide"), None),
            P("req", "wide", None),
            P("req", "wide", None),
            P("req"),
            P("req", "wide"),
            P("req"),
        ),
        out_specs=(P(("req", "wide"), None), P("req", "wide"), P("req", "wide"), P("req", "wide")),
        check_vma=False,
    )
```

```python
import jax
import jax.numpy as jnp
from jax import lax
from jax.sharding import PartitionSpec as P

D = 7168
HEADS = 32
HD = 224
RANK = 128
SPAN = 128


EPSILON = 1e-05
NEG_LARGE = -1e30
WIDE = ("chip", "core")
HALF = ("req", "chip")


def rms_scale(values, gains):
    widened = values.astype(jnp.float32)
    meansq = jnp.mean(widened * widened, axis=-1, keepdims=True)
    return (widened * lax.rsqrt(meansq + EPSILON) * gains.astype(jnp.float32)).astype(jnp.bfloat16)


def gather_rows(piece, axis, count):
    spread = jnp.broadcast_to(piece[None], (count,) + piece.shape)
    return lax.all_to_all(spread, axis, 0, 0, tiled=True)


def send_rows(values, axis, count):
    blocks = values.reshape((count, values.shape[0] // count) + values.shape[1:])
    return lax.all_to_all(blocks, axis, 0, 0, tiled=True)


def split_pair(values):
    high = lax.reduce_precision(values, exponent_bits=8, mantissa_bits=7)
    low = lax.reduce_precision(values - high, exponent_bits=8, mantissa_bits=7)
    return high, low


def join_pair(high, low):
    return high.astype(jnp.float32) + low.astype(jnp.float32)


def body(
    tokens,
    attn_gain,
    qkv_weight,
    adapter_down,
    adapter_up,
    out_weight,
    mlp_gain,
    gate_up,
    down_weight,
    key_cache,
    value_cache,
    cache_lengths,
    slot_mask,
    span_counts,
):
    score_scale = HD ** (-0.5)
    wide_size = lax.psum(1, WIDE)
    half_size = lax.psum(1, HALF)
    local_width = qkv_weight.shape[2]
    local_heads = local_width // HD
    own_rows = tokens.shape[0]
    wide_index = lax.axis_index(WIDE)
    feature_start = wide_index * local_width

    swap = [(0, 1), (1, 0)]
    chip_gate = jnp.concatenate([gate_up, lax.ppermute(gate_up, "core", swap)], axis=1)
    chip_down = jnp.concatenate([down_weight, lax.ppermute(down_weight, "core", swap)], axis=0)

    normed = rms_scale(tokens, attn_gain)
    shard_rows = gather_rows(normed, WIDE, wide_size).reshape(SPAN, D)
    base_part = jnp.dot(
        shard_rows, qkv_weight.reshape(D, 3 * local_width), preferred_element_type=jnp.float32
    )
    sliced = lax.dynamic_slice_in_dim(shard_rows, feature_start, local_width, 1)
    partial_low = jnp.dot(sliced, adapter_down, preferred_element_type=jnp.float32)
    low_parts = send_rows(partial_low, WIDE, wide_size)
    own_low = jnp.sum(low_parts, axis=0).astype(jnp.bfloat16)
    lowrank = gather_rows(own_low, WIDE, wide_size).reshape(SPAN, 3, RANK)
    adapted = jnp.einsum("tcr,crd->tcd", lowrank, adapter_up, preferred_element_type=jnp.float32)
    projected = (base_part.reshape(SPAN, 3, local_width) + adapted).astype(jnp.bfloat16)
    query_own = projected[:, 0]
    new_keys = projected[:, 1]
    new_values = projected[:, 2]

    query_heads = gather_rows(query_own, WIDE, wide_size).reshape(HEADS, SPAN, HD)
    block_len = key_cache.shape[1]
    block_start = wide_index * block_len
    length = cache_lengths[0]
    usable = (block_start + jnp.arange(block_len) < length) & (slot_mask[0] == 1)

    def cache_block(unused):
        key_heads = key_cache[0].reshape(block_len, HEADS, HD)
        value_heads = value_cache[0].reshape(block_len, HEADS, HD)
        scores = (
            jnp.einsum("hqd,khd->hqk", query_heads, key_heads, preferred_element_type=jnp.float32)
            * score_scale
        )
        scores = jnp.where(usable, scores, NEG_LARGE)
        highest = jnp.max(scores, axis=-1)
        high, low = split_pair(highest)
        reference_max = high + low
        weights = jnp.where(usable, jnp.exp(scores - reference_max[..., None]), 0.0)
        totals = jnp.sum(weights, axis=-1)
        numerator = jnp.einsum(
            "hqk,khd->hqd",
            weights.astype(jnp.bfloat16),
            value_heads,
            preferred_element_type=jnp.float32,
        )
        total_high, total_low = split_pair(totals)
        stats = jnp.stack([high, low, total_high, total_low], axis=-1).astype(jnp.bfloat16)
        return jnp.concatenate([numerator.astype(jnp.bfloat16), stats], axis=-1)

    def skipped(unused):
        stats = jnp.zeros((HEADS, SPAN, 4), jnp.bfloat16).at[..., 0].set(NEG_LARGE)
        return jnp.concatenate([jnp.zeros((HEADS, SPAN, HD), jnp.bfloat16), stats], axis=-1)

    packed = lax.cond(block_start < length, cache_block, skipped, 0)
    parts = lax.all_to_all(packed, WIDE, 0, 0, tiled=True)
    part_num = parts[..., :HD].astype(jnp.float32)
    part_max = join_pair(parts[..., HD], parts[..., HD + 1])
    part_sum = join_pair(parts[..., HD + 2], parts[..., HD + 3])

    span_count = span_counts[0]
    query_pos = jnp.arange(SPAN)[:, None]
    key_pos = jnp.arange(SPAN)[None, :]
    span_ok = ((key_pos <= query_pos) & ((key_pos < span_count) | (key_pos == query_pos)))[
        :, None, :
    ]
    own_query = query_own.reshape(SPAN, local_heads, HD)
    own_keys = new_keys.reshape(SPAN, local_heads, HD)
    own_values = new_values.reshape(SPAN, local_heads, HD)
    own_scores = (
        jnp.einsum("qhd,khd->qhk", own_query, own_keys, preferred_element_type=jnp.float32)
        * score_scale
    )
    own_scores = jnp.where(span_ok, own_scores, NEG_LARGE)
    own_max = jnp.max(own_scores, axis=-1)
    own_weights = jnp.where(span_ok, jnp.exp(own_scores - own_max[..., None]), 0.0)
    own_sum = jnp.sum(own_weights, axis=-1)
    own_num = jnp.einsum(
        "qhk,khd->qhd",
        own_weights.astype(jnp.bfloat16),
        own_values,
        preferred_element_type=jnp.float32,
    )
    own_num = own_num.reshape(SPAN, HD)
    own_max = own_max.reshape(SPAN)
    own_sum = own_sum.reshape(SPAN)

    highest = jnp.maximum(jnp.max(part_max, axis=0), own_max)
    part_factor = jnp.exp(part_max - highest)
    own_factor = jnp.exp(own_max - highest)
    numerator = jnp.sum(part_num * part_factor[..., None], axis=0) + own_num * own_factor[:, None]
    totals = jnp.sum(part_sum * part_factor, axis=0) + own_sum * own_factor
    attention = (numerator / totals[:, None]).astype(jnp.bfloat16)

    head_out = jnp.dot(attention, out_weight, preferred_element_type=jnp.float32)
    out_parts = send_rows(head_out.astype(jnp.bfloat16), WIDE, wide_size)
    attn_out = jnp.sum(out_parts.astype(jnp.float32), axis=0)
    normed_mid = rms_scale(attn_out, mlp_gain)
    half_rows = gather_rows(normed_mid, HALF, half_size).reshape(half_size * own_rows, -1)
    both = jnp.einsum("td,cfd->ctf", half_rows, chip_gate, preferred_element_type=jnp.float32)
    hidden = (jax.nn.silu(both[0]) * both[1]).astype(jnp.bfloat16)
    ffn_part = jnp.dot(hidden, chip_down, preferred_element_type=jnp.float32)
    ffn_parts = send_rows(ffn_part.astype(jnp.bfloat16), HALF, half_size)
    hidden_out = jnp.sum(ffn_parts.astype(jnp.float32), axis=0).astype(jnp.bfloat16)
    return (hidden_out, attention, new_keys, new_values)


def solution(mesh):
    chips = mesh.shape["wide"] // 2
    split_mesh = jax.sharding.Mesh(
        mesh.devices.reshape(mesh.shape["req"], chips, 2), ("req", "chip", "core")
    )
    return jax.shard_map(
        body,
        mesh=split_mesh,
        in_specs=(
            P(("req",) + WIDE, None),
            P(),
            P(None, None, WIDE),
            P(WIDE, None),
            P(None, None, WIDE),
            P(WIDE, None),
            P(),
            P(None, ("req",) + WIDE, None),
            P(("req",) + WIDE, None),
            P("req", WIDE, None),
            P("req", WIDE, None),
            P("req"),
            P("req", WIDE),
            P("req"),
        ),
        out_specs=(P(("req",) + WIDE, None), P("req", WIDE), P("req", WIDE), P("req", WIDE)),
        check_vma=False,
    )
```

```python
import jax
import jax.numpy as jnp
from jax import lax
from jax.sharding import PartitionSpec as P

D = 7168
HEADS = 32
HD = 224
RANK = 128
SPAN = 128


EPSILON = 1e-05
NEG_LARGE = -1e30
WIDE = ("chip", "core")
HALF = ("req", "chip")


def rms_scale(values, gains):
    widened = values.astype(jnp.float32)
    meansq = jnp.mean(widened * widened, axis=-1, keepdims=True)
    return (widened * lax.rsqrt(meansq + EPSILON) * gains.astype(jnp.float32)).astype(jnp.bfloat16)


def gather_rows(piece, axis, count):
    spread = jnp.broadcast_to(piece[None], (count,) + piece.shape)
    return lax.all_to_all(spread, axis, 0, 0, tiled=True)


def gather_wide(piece, chips):
    own = gather_rows(piece, "chip", chips)
    other = lax.ppermute(own, "core", [(0, 1), (1, 0)])
    first_core = lax.axis_index("core") == 0
    even = jnp.where(first_core, own, other)
    odd = jnp.where(first_core, other, own)
    joined = jnp.stack([even, odd], axis=1)
    return joined.reshape((2 * chips,) + piece.shape)


def send_rows(values, axis, count):
    blocks = values.reshape((count, values.shape[0] // count) + values.shape[1:])
    return lax.all_to_all(blocks, axis, 0, 0, tiled=True)


def split_pair(values):
    high = lax.reduce_precision(values, exponent_bits=8, mantissa_bits=7)
    low = lax.reduce_precision(values - high, exponent_bits=8, mantissa_bits=7)
    return high, low


def join_pair(high, low):
    return high.astype(jnp.float32) + low.astype(jnp.float32)


def body(
    tokens,
    attn_gain,
    qkv_weight,
    adapter_down,
    adapter_up,
    out_weight,
    mlp_gain,
    gate_up,
    down_weight,
    key_cache,
    value_cache,
    cache_lengths,
    slot_mask,
    span_counts,
):
    score_scale = HD ** (-0.5)
    wide_size = lax.psum(1, WIDE)
    half_size = lax.psum(1, HALF)
    chips = lax.psum(1, "chip")
    local_width = qkv_weight.shape[2]
    local_heads = local_width // HD
    own_rows = tokens.shape[0]
    wide_index = lax.axis_index(WIDE)
    feature_start = wide_index * local_width

    swap = [(0, 1), (1, 0)]
    chip_gate = jnp.concatenate([gate_up, lax.ppermute(gate_up, "core", swap)], axis=1)
    chip_down = jnp.concatenate([down_weight, lax.ppermute(down_weight, "core", swap)], axis=0)

    normed = rms_scale(tokens, attn_gain)
    shard_rows = gather_wide(normed, chips).reshape(SPAN, D)
    base_part = jnp.dot(
        shard_rows, qkv_weight.reshape(D, 3 * local_width), preferred_element_type=jnp.float32
    )
    sliced = lax.dynamic_slice_in_dim(shard_rows, feature_start, local_width, 1)
    partial_low = jnp.dot(sliced, adapter_down, preferred_element_type=jnp.float32)
    low_parts = send_rows(partial_low, WIDE, wide_size)
    own_low = jnp.sum(low_parts, axis=0).astype(jnp.bfloat16)
    lowrank = gather_rows(own_low, WIDE, wide_size).reshape(SPAN, 3, RANK)
    adapted = jnp.einsum("tcr,crd->tcd", lowrank, adapter_up, preferred_element_type=jnp.float32)
    projected = (base_part.reshape(SPAN, 3, local_width) + adapted).astype(jnp.bfloat16)
    query_own = projected[:, 0]
    new_keys = projected[:, 1]
    new_values = projected[:, 2]

    query_heads = gather_wide(query_own, chips).reshape(HEADS, SPAN, HD)
    block_len = key_cache.shape[1]
    block_start = wide_index * block_len
    length = cache_lengths[0]
    usable = (block_start + jnp.arange(block_len) < length) & (slot_mask[0] == 1)

    def cache_block(unused):
        key_heads = key_cache[0].reshape(block_len, HEADS, HD)
        value_heads = value_cache[0].reshape(block_len, HEADS, HD)
        scores = (
            jnp.einsum("hqd,khd->hqk", query_heads, key_heads, preferred_element_type=jnp.float32)
            * score_scale
        )
        scores = jnp.where(usable, scores, NEG_LARGE)
        highest = jnp.max(scores, axis=-1)
        high, low = split_pair(highest)
        reference_max = high + low
        weights = jnp.where(usable, jnp.exp(scores - reference_max[..., None]), 0.0)
        totals = jnp.sum(weights, axis=-1)
        numerator = jnp.einsum(
            "hqk,khd->hqd",
            weights.astype(jnp.bfloat16),
            value_heads,
            preferred_element_type=jnp.float32,
        )
        total_high, total_low = split_pair(totals)
        stats = jnp.stack([high, low, total_high, total_low], axis=-1).astype(jnp.bfloat16)
        return jnp.concatenate([numerator.astype(jnp.bfloat16), stats], axis=-1)

    def skipped(unused):
        stats = jnp.zeros((HEADS, SPAN, 4), jnp.bfloat16).at[..., 0].set(NEG_LARGE)
        return jnp.concatenate([jnp.zeros((HEADS, SPAN, HD), jnp.bfloat16), stats], axis=-1)

    packed = lax.cond(block_start < length, cache_block, skipped, 0)
    parts = lax.all_to_all(packed, WIDE, 0, 0, tiled=True)
    part_num = parts[..., :HD].astype(jnp.float32)
    part_max = join_pair(parts[..., HD], parts[..., HD + 1])
    part_sum = join_pair(parts[..., HD + 2], parts[..., HD + 3])

    span_count = span_counts[0]
    query_pos = jnp.arange(SPAN)[:, None]
    key_pos = jnp.arange(SPAN)[None, :]
    span_ok = ((key_pos <= query_pos) & ((key_pos < span_count) | (key_pos == query_pos)))[
        :, None, :
    ]
    own_query = query_own.reshape(SPAN, local_heads, HD)
    own_keys = new_keys.reshape(SPAN, local_heads, HD)
    own_values = new_values.reshape(SPAN, local_heads, HD)
    own_scores = (
        jnp.einsum("qhd,khd->qhk", own_query, own_keys, preferred_element_type=jnp.float32)
        * score_scale
    )
    own_scores = jnp.where(span_ok, own_scores, NEG_LARGE)
    own_max = jnp.max(own_scores, axis=-1)
    own_weights = jnp.where(span_ok, jnp.exp(own_scores - own_max[..., None]), 0.0)
    own_sum = jnp.sum(own_weights, axis=-1)
    own_num = jnp.einsum(
        "qhk,khd->qhd",
        own_weights.astype(jnp.bfloat16),
        own_values,
        preferred_element_type=jnp.float32,
    )
    own_num = own_num.reshape(SPAN, HD)
    own_max = own_max.reshape(SPAN)
    own_sum = own_sum.reshape(SPAN)

    highest = jnp.maximum(jnp.max(part_max, axis=0), own_max)
    part_factor = jnp.exp(part_max - highest)
    own_factor = jnp.exp(own_max - highest)
    numerator = jnp.sum(part_num * part_factor[..., None], axis=0) + own_num * own_factor[:, None]
    totals = jnp.sum(part_sum * part_factor, axis=0) + own_sum * own_factor
    attention = (numerator / totals[:, None]).astype(jnp.bfloat16)

    head_out = jnp.dot(attention, out_weight, preferred_element_type=jnp.float32)
    out_parts = send_rows(head_out.astype(jnp.bfloat16), WIDE, wide_size)
    attn_out = jnp.sum(out_parts.astype(jnp.float32), axis=0)
    normed_mid = rms_scale(attn_out, mlp_gain)
    half_rows = gather_rows(normed_mid, HALF, half_size).reshape(half_size * own_rows, -1)
    both = jnp.einsum("td,cfd->ctf", half_rows, chip_gate, preferred_element_type=jnp.float32)
    hidden = (jax.nn.silu(both[0]) * both[1]).astype(jnp.bfloat16)
    ffn_part = jnp.dot(hidden, chip_down, preferred_element_type=jnp.float32)
    ffn_parts = send_rows(ffn_part.astype(jnp.bfloat16), HALF, half_size)
    hidden_out = jnp.sum(ffn_parts.astype(jnp.float32), axis=0).astype(jnp.bfloat16)
    return (hidden_out, attention, new_keys, new_values)


def solution(mesh):
    chips = mesh.shape["wide"] // 2
    split_mesh = jax.sharding.Mesh(
        mesh.devices.reshape(mesh.shape["req"], chips, 2), ("req", "chip", "core")
    )
    return jax.shard_map(
        body,
        mesh=split_mesh,
        in_specs=(
            P(("req",) + WIDE, None),
            P(),
            P(None, None, WIDE),
            P(WIDE, None),
            P(None, None, WIDE),
            P(WIDE, None),
            P(),
            P(None, ("req",) + WIDE, None),
            P(("req",) + WIDE, None),
            P("req", WIDE, None),
            P("req", WIDE, None),
            P("req"),
            P("req", WIDE),
            P("req"),
        ),
        out_specs=(P(("req",) + WIDE, None), P("req", WIDE), P("req", WIDE), P("req", WIDE)),
        check_vma=False,
    )
```

```python
import jax
import jax.numpy as jnp
from jax import lax
from jax.sharding import PartitionSpec as P

D = 7168
HEADS = 32
HD = 224
RANK = 128
SPAN = 128


EPSILON = 1e-05
NEG_LARGE = -1e30
WIDE = ("chip", "core")
HALF = ("req", "chip")


def rms_scale(values, gains):
    widened = values.astype(jnp.float32)
    meansq = jnp.mean(widened * widened, axis=-1, keepdims=True)
    return (widened * lax.rsqrt(meansq + EPSILON) * gains.astype(jnp.float32)).astype(jnp.bfloat16)


def gather_rows(piece, axis, count):
    spread = jnp.broadcast_to(piece[None], (count,) + piece.shape)
    return lax.all_to_all(spread, axis, 0, 0, tiled=True)


def gather_wide(piece, chips):
    own = gather_rows(piece, "chip", chips)
    other = lax.ppermute(own, "core", [(0, 1), (1, 0)])
    first_core = lax.axis_index("core") == 0
    even = jnp.where(first_core, own, other)
    odd = jnp.where(first_core, other, own)
    joined = jnp.stack([even, odd], axis=1)
    return joined.reshape((2 * chips,) + piece.shape)


def send_rows(values, axis, count):
    blocks = values.reshape((count, values.shape[0] // count) + values.shape[1:])
    return lax.all_to_all(blocks, axis, 0, 0, tiled=True)


def split_pair(values):
    high = lax.reduce_precision(values, exponent_bits=8, mantissa_bits=7)
    low = lax.reduce_precision(values - high, exponent_bits=8, mantissa_bits=7)
    return high, low


def join_pair(high, low):
    return high.astype(jnp.float32) + low.astype(jnp.float32)


def body(
    tokens,
    attn_gain,
    qkv_weight,
    adapter_down,
    adapter_up,
    out_weight,
    mlp_gain,
    gate_up,
    down_weight,
    key_cache,
    value_cache,
    cache_lengths,
    slot_mask,
    span_counts,
):
    score_scale = HD ** (-0.5)
    wide_size = lax.psum(1, WIDE)
    half_size = lax.psum(1, HALF)
    chips = lax.psum(1, "chip")
    local_width = qkv_weight.shape[2]
    local_heads = local_width // HD
    own_rows = tokens.shape[0]
    wide_index = lax.axis_index(WIDE)
    feature_start = wide_index * local_width

    swap = [(0, 1), (1, 0)]
    chip_gate = jnp.concatenate([gate_up, lax.ppermute(gate_up, "core", swap)], axis=1)
    chip_down = jnp.concatenate([down_weight, lax.ppermute(down_weight, "core", swap)], axis=0)

    normed = rms_scale(tokens, attn_gain)
    shard_rows = gather_wide(normed, chips).reshape(SPAN, D)
    base_part = lax.optimization_barrier(
        jnp.dot(shard_rows, qkv_weight.reshape(D, 3 * local_width), preferred_element_type=jnp.float32)
    )
    sliced = lax.dynamic_slice_in_dim(shard_rows, feature_start, local_width, 1)
    partial_low = jnp.dot(sliced, adapter_down, preferred_element_type=jnp.float32)
    low_parts = send_rows(partial_low, WIDE, wide_size)
    own_low = jnp.sum(low_parts, axis=0).astype(jnp.bfloat16)
    lowrank = gather_rows(own_low, WIDE, wide_size).reshape(SPAN, 3, RANK)
    adapted = jnp.einsum("tcr,crd->tcd", lowrank, adapter_up, preferred_element_type=jnp.float32)
    projected = (base_part.reshape(SPAN, 3, local_width) + adapted).astype(jnp.bfloat16)
    query_own = projected[:, 0]
    new_keys = projected[:, 1]
    new_values = projected[:, 2]

    query_heads = gather_wide(query_own, chips).reshape(HEADS, SPAN, HD)
    block_len = key_cache.shape[1]
    block_start = wide_index * block_len
    length = cache_lengths[0]
    usable = (block_start + jnp.arange(block_len) < length) & (slot_mask[0] == 1)

    key_heads = jnp.transpose(key_cache[0].reshape(block_len, HEADS, HD), (1, 0, 2))
    value_heads = jnp.transpose(value_cache[0].reshape(block_len, HEADS, HD), (1, 0, 2))

    def cache_block(unused):
        scores = (
            jnp.einsum("hqd,hkd->hqk", query_heads, key_heads, preferred_element_type=jnp.float32)
            * score_scale
        )
        scores = jnp.where(usable, scores, NEG_LARGE)
        highest = jnp.max(scores, axis=-1)
        high, low = split_pair(highest)
        reference_max = high + low
        weights = jnp.where(usable, jnp.exp(scores - reference_max[..., None]), 0.0)
        totals = jnp.sum(weights, axis=-1)
        numerator = jnp.einsum(
            "hqk,hkd->hqd",
            weights.astype(jnp.bfloat16),
            value_heads,
            preferred_element_type=jnp.float32,
        )
        total_high, total_low = split_pair(totals)
        stats = jnp.stack([high, low, total_high, total_low], axis=-1).astype(jnp.bfloat16)
        return jnp.concatenate([numerator.astype(jnp.bfloat16), stats], axis=-1)

    def skipped(unused):
        stats = jnp.zeros((HEADS, SPAN, 4), jnp.bfloat16).at[..., 0].set(NEG_LARGE)
        return jnp.concatenate([jnp.zeros((HEADS, SPAN, HD), jnp.bfloat16), stats], axis=-1)

    packed = lax.cond(block_start < length, cache_block, skipped, 0)
    parts = lax.all_to_all(packed, WIDE, 0, 0, tiled=True)
    part_num = parts[..., :HD].astype(jnp.float32)
    part_max = join_pair(parts[..., HD], parts[..., HD + 1])
    part_sum = join_pair(parts[..., HD + 2], parts[..., HD + 3])

    span_count = span_counts[0]
    query_pos = jnp.arange(SPAN)[:, None]
    key_pos = jnp.arange(SPAN)[None, :]
    span_ok = ((key_pos <= query_pos) & ((key_pos < span_count) | (key_pos == query_pos)))[
        :, None, :
    ]
    own_query = query_own.reshape(SPAN, local_heads, HD)
    own_keys = new_keys.reshape(SPAN, local_heads, HD)
    own_values = new_values.reshape(SPAN, local_heads, HD)
    own_scores = (
        jnp.einsum("qhd,khd->qhk", own_query, own_keys, preferred_element_type=jnp.float32)
        * score_scale
    )
    own_scores = jnp.where(span_ok, own_scores, NEG_LARGE)
    own_max = jnp.max(own_scores, axis=-1)
    own_weights = jnp.where(span_ok, jnp.exp(own_scores - own_max[..., None]), 0.0)
    own_sum = jnp.sum(own_weights, axis=-1)
    own_num = jnp.einsum(
        "qhk,khd->qhd",
        own_weights.astype(jnp.bfloat16),
        own_values,
        preferred_element_type=jnp.float32,
    )
    own_num = own_num.reshape(SPAN, HD)
    own_max = own_max.reshape(SPAN)
    own_sum = own_sum.reshape(SPAN)

    highest = jnp.maximum(jnp.max(part_max, axis=0), own_max)
    part_factor = jnp.exp(part_max - highest)
    own_factor = jnp.exp(own_max - highest)
    numerator = jnp.sum(part_num * part_factor[..., None], axis=0) + own_num * own_factor[:, None]
    totals = jnp.sum(part_sum * part_factor, axis=0) + own_sum * own_factor
    attention = (numerator / totals[:, None]).astype(jnp.bfloat16)

    head_out = jnp.dot(attention, out_weight, preferred_element_type=jnp.float32)
    out_parts = send_rows(head_out.astype(jnp.bfloat16), WIDE, wide_size)
    attn_out = jnp.sum(out_parts.astype(jnp.float32), axis=0)
    normed_mid = rms_scale(attn_out, mlp_gain)
    half_rows = gather_rows(normed_mid, HALF, half_size).reshape(half_size * own_rows, -1)
    both = jnp.einsum("td,cfd->ctf", half_rows, chip_gate, preferred_element_type=jnp.float32)
    hidden = (jax.nn.silu(both[0]) * both[1]).astype(jnp.bfloat16)
    ffn_part = jnp.dot(hidden, chip_down, preferred_element_type=jnp.float32)
    ffn_parts = send_rows(ffn_part.astype(jnp.bfloat16), HALF, half_size)
    hidden_out = jnp.sum(ffn_parts.astype(jnp.float32), axis=0).astype(jnp.bfloat16)
    return (hidden_out, attention, new_keys, new_values)


def solution(mesh):
    chips = mesh.shape["wide"] // 2
    split_mesh = jax.sharding.Mesh(
        mesh.devices.reshape(mesh.shape["req"], chips, 2), ("req", "chip", "core")
    )
    return jax.shard_map(
        body,
        mesh=split_mesh,
        in_specs=(
            P(("req",) + WIDE, None),
            P(),
            P(None, None, WIDE),
            P(WIDE, None),
            P(None, None, WIDE),
            P(WIDE, None),
            P(),
            P(None, ("req",) + WIDE, None),
            P(("req",) + WIDE, None),
            P("req", WIDE, None),
            P("req", WIDE, None),
            P("req"),
            P("req", WIDE),
            P("req"),
        ),
        out_specs=(P(("req",) + WIDE, None), P("req", WIDE), P("req", WIDE), P("req", WIDE)),
        check_vma=False,
    )
```

```python
import jax
import jax.numpy as jnp
from jax import lax
from jax.sharding import PartitionSpec as P

D = 7168
HEADS = 32
HD = 224
RANK = 128
SPAN = 128


EPSILON = 1e-05
NEG_LARGE = -1e30
WIDE = ("chip", "core")
HALF = ("req", "chip")


def rms_scale(values, gains):
    widened = values.astype(jnp.float32)
    meansq = jnp.mean(widened * widened, axis=-1, keepdims=True)
    return (widened * lax.rsqrt(meansq + EPSILON) * gains.astype(jnp.float32)).astype(jnp.bfloat16)


def gather_rows(piece, axis, count):
    spread = jnp.broadcast_to(piece[None], (count,) + piece.shape)
    return lax.all_to_all(spread, axis, 0, 0, tiled=True)


def gather_wide(piece, chips):
    own = gather_rows(piece, "chip", chips)[:, None]
    other = lax.ppermute(own, "core", [(0, 1), (1, 0)])
    core = lax.axis_index("core")
    joined = jnp.zeros((chips, 2) + piece.shape, piece.dtype)
    joined = lax.dynamic_update_slice_in_dim(joined, own, core, axis=1)
    joined = lax.dynamic_update_slice_in_dim(joined, other, 1 - core, axis=1)
    return joined.reshape((2 * chips,) + piece.shape)


def send_rows(values, axis, count):
    blocks = values.reshape((count, values.shape[0] // count) + values.shape[1:])
    return lax.all_to_all(blocks, axis, 0, 0, tiled=True)


def split_pair(values):
    high = lax.reduce_precision(values, exponent_bits=8, mantissa_bits=7)
    low = lax.reduce_precision(values - high, exponent_bits=8, mantissa_bits=7)
    return high, low


def join_pair(high, low):
    return high.astype(jnp.float32) + low.astype(jnp.float32)


def body(
    tokens,
    attn_gain,
    qkv_weight,
    adapter_down,
    adapter_up,
    out_weight,
    mlp_gain,
    gate_up,
    down_weight,
    key_cache,
    value_cache,
    cache_lengths,
    slot_mask,
    span_counts,
):
    score_scale = HD ** (-0.5)
    wide_size = lax.psum(1, WIDE)
    half_size = lax.psum(1, HALF)
    chips = lax.psum(1, "chip")
    local_width = qkv_weight.shape[2]
    local_heads = local_width // HD
    own_rows = tokens.shape[0]
    wide_index = lax.axis_index(WIDE)
    feature_start = wide_index * local_width

    swap = [(0, 1), (1, 0)]
    chip_gate = jnp.concatenate([gate_up, lax.ppermute(gate_up, "core", swap)], axis=1)
    chip_down = jnp.concatenate([down_weight, lax.ppermute(down_weight, "core", swap)], axis=0)

    normed = rms_scale(tokens, attn_gain)
    shard_rows = gather_wide(normed, chips).reshape(SPAN, D)
    block_len = key_cache.shape[1]
    key_heads = jnp.transpose(key_cache[0].reshape(block_len, HEADS, HD), (1, 0, 2))
    value_heads = jnp.transpose(value_cache[0].reshape(block_len, HEADS, HD), (1, 0, 2))
    shard_rows, key_heads, value_heads = lax.optimization_barrier((shard_rows, key_heads, value_heads))
    base_part = lax.optimization_barrier(
        jnp.dot(shard_rows, qkv_weight.reshape(D, 3 * local_width), preferred_element_type=jnp.float32)
    )
    sliced = lax.dynamic_slice_in_dim(shard_rows, feature_start, local_width, 1)
    partial_low = jnp.dot(sliced, adapter_down, preferred_element_type=jnp.float32)
    low_parts = send_rows(partial_low.astype(jnp.bfloat16), WIDE, wide_size)
    own_low = jnp.sum(low_parts.astype(jnp.float32), axis=0).astype(jnp.bfloat16)
    lowrank = gather_rows(own_low, WIDE, wide_size).reshape(SPAN, 3, RANK)
    adapted = jnp.einsum("tcr,crd->tcd", lowrank, adapter_up, preferred_element_type=jnp.float32)
    projected = (base_part.reshape(SPAN, 3, local_width) + adapted).astype(jnp.bfloat16)
    query_own = projected[:, 0]
    new_keys = projected[:, 1]
    new_values = projected[:, 2]

    query_heads = gather_wide(query_own, chips).reshape(HEADS, SPAN, HD)
    block_start = wide_index * block_len
    length = cache_lengths[0]
    usable = (block_start + jnp.arange(block_len) < length) & (slot_mask[0] == 1)


    def cache_block(unused):
        scores = (
            jnp.einsum("hqd,hkd->hqk", query_heads, key_heads, preferred_element_type=jnp.float32)
            * score_scale
        )
        scores = jnp.where(usable, scores, NEG_LARGE)
        highest = jnp.max(scores, axis=-1)
        high, low = split_pair(highest)
        reference_max = high + low
        weights = jnp.where(usable, jnp.exp(scores - reference_max[..., None]), 0.0)
        totals = jnp.sum(weights, axis=-1)
        numerator = jnp.einsum(
            "hqk,hkd->hqd",
            weights.astype(jnp.bfloat16),
            value_heads,
            preferred_element_type=jnp.float32,
        )
        total_high, total_low = split_pair(totals)
        stats = jnp.stack([high, low, total_high, total_low], axis=-1).astype(jnp.bfloat16)
        return jnp.concatenate([numerator.astype(jnp.bfloat16), stats], axis=-1)

    def skipped(unused):
        stats = jnp.zeros((HEADS, SPAN, 4), jnp.bfloat16).at[..., 0].set(NEG_LARGE)
        return jnp.concatenate([jnp.zeros((HEADS, SPAN, HD), jnp.bfloat16), stats], axis=-1)

    packed = lax.cond(block_start < length, cache_block, skipped, 0)
    parts = lax.all_to_all(packed, WIDE, 0, 0, tiled=True)
    part_num = parts[..., :HD].astype(jnp.float32)
    part_max = join_pair(parts[..., HD], parts[..., HD + 1])
    part_sum = join_pair(parts[..., HD + 2], parts[..., HD + 3])

    span_count = span_counts[0]
    query_pos = jnp.arange(SPAN)[:, None]
    key_pos = jnp.arange(SPAN)[None, :]
    span_ok = ((key_pos <= query_pos) & ((key_pos < span_count) | (key_pos == query_pos)))[
        :, None, :
    ]
    own_query = query_own.reshape(SPAN, local_heads, HD)
    own_keys = new_keys.reshape(SPAN, local_heads, HD)
    own_values = new_values.reshape(SPAN, local_heads, HD)
    own_scores = (
        jnp.einsum("qhd,khd->qhk", own_query, own_keys, preferred_element_type=jnp.float32)
        * score_scale
    )
    own_scores = jnp.where(span_ok, own_scores, NEG_LARGE)
    own_max = jnp.max(own_scores, axis=-1)
    own_weights = jnp.where(span_ok, jnp.exp(own_scores - own_max[..., None]), 0.0)
    own_sum = jnp.sum(own_weights, axis=-1)
    own_num = jnp.einsum(
        "qhk,khd->qhd",
        own_weights.astype(jnp.bfloat16),
        own_values,
        preferred_element_type=jnp.float32,
    )
    own_num = own_num.reshape(SPAN, HD)
    own_max = own_max.reshape(SPAN)
    own_sum = own_sum.reshape(SPAN)

    highest = jnp.maximum(jnp.max(part_max, axis=0), own_max)
    part_factor = jnp.exp(part_max - highest)
    own_factor = jnp.exp(own_max - highest)
    numerator = jnp.sum(part_num * part_factor[..., None], axis=0) + own_num * own_factor[:, None]
    totals = jnp.sum(part_sum * part_factor, axis=0) + own_sum * own_factor
    attention = (numerator / totals[:, None]).astype(jnp.bfloat16)

    head_out = jnp.dot(attention, out_weight, preferred_element_type=jnp.float32)
    out_parts = send_rows(head_out.astype(jnp.bfloat16), WIDE, wide_size)
    attn_out = jnp.sum(out_parts.astype(jnp.float32), axis=0)
    normed_mid = rms_scale(attn_out, mlp_gain)
    half_rows = gather_rows(normed_mid, HALF, half_size).reshape(half_size * own_rows, -1)
    both = jnp.einsum("td,cfd->ctf", half_rows, chip_gate, preferred_element_type=jnp.float32)
    hidden = (jax.nn.silu(both[0]) * both[1]).astype(jnp.bfloat16)
    ffn_part = jnp.dot(hidden, chip_down, preferred_element_type=jnp.float32)
    ffn_parts = send_rows(ffn_part.astype(jnp.bfloat16), HALF, half_size)
    hidden_out = jnp.sum(ffn_parts.astype(jnp.float32), axis=0).astype(jnp.bfloat16)
    return (hidden_out, attention, new_keys, new_values)


def solution(mesh):
    chips = mesh.shape["wide"] // 2
    split_mesh = jax.sharding.Mesh(
        mesh.devices.reshape(mesh.shape["req"], chips, 2), ("req", "chip", "core")
    )
    return jax.shard_map(
        body,
        mesh=split_mesh,
        in_specs=(
            P(("req",) + WIDE, None),
            P(),
            P(None, None, WIDE),
            P(WIDE, None),
            P(None, None, WIDE),
            P(WIDE, None),
            P(),
            P(None, ("req",) + WIDE, None),
            P(("req",) + WIDE, None),
            P("req", WIDE, None),
            P("req", WIDE, None),
            P("req"),
            P("req", WIDE),
            P("req"),
        ),
        out_specs=(P(("req",) + WIDE, None), P("req", WIDE), P("req", WIDE), P("req", WIDE)),
        check_vma=False,
    )
```

```python
import jax
import jax.numpy as jnp
from jax import lax
from jax.sharding import PartitionSpec as P

D = 7168
HEADS = 32
HD = 224
RANK = 128
SPAN = 128


EPSILON = 1e-05
NEG_LARGE = -1e30
WIDE = ("chip", "core")
HALF = ("req", "chip")


def rms_scale(values, gains):
    widened = values.astype(jnp.float32)
    meansq = jnp.mean(widened * widened, axis=-1, keepdims=True)
    return (widened * lax.rsqrt(meansq + EPSILON) * gains.astype(jnp.float32)).astype(jnp.bfloat16)


def gather_rows(piece, axis, count):
    spread = jnp.broadcast_to(piece[None], (count,) + piece.shape)
    return lax.all_to_all(spread, axis, 0, 0, tiled=True)


def gather_wide(piece, chips):
    own = gather_rows(piece, "chip", chips)[:, None]
    other = lax.ppermute(own, "core", [(0, 1), (1, 0)])
    core = lax.axis_index("core")
    joined = jnp.zeros((chips, 2) + piece.shape, piece.dtype)
    joined = lax.dynamic_update_slice_in_dim(joined, own, core, axis=1)
    joined = lax.dynamic_update_slice_in_dim(joined, other, 1 - core, axis=1)
    return joined.reshape((2 * chips,) + piece.shape)


def send_rows(values, axis, count):
    blocks = values.reshape((count, values.shape[0] // count) + values.shape[1:])
    return lax.all_to_all(blocks, axis, 0, 0, tiled=True)


def split_pair(values):
    high = lax.reduce_precision(values, exponent_bits=8, mantissa_bits=7)
    low = lax.reduce_precision(values - high, exponent_bits=8, mantissa_bits=7)
    return high, low


def join_pair(high, low):
    return high.astype(jnp.float32) + low.astype(jnp.float32)


def body(
    tokens,
    attn_gain,
    qkv_weight,
    adapter_down,
    adapter_up,
    out_weight,
    mlp_gain,
    gate_up,
    down_weight,
    key_cache,
    value_cache,
    cache_lengths,
    slot_mask,
    span_counts,
):
    score_scale = HD ** (-0.5)
    wide_size = lax.psum(1, WIDE)
    half_size = lax.psum(1, HALF)
    chips = lax.psum(1, "chip")
    local_width = qkv_weight.shape[2]
    local_heads = local_width // HD
    own_rows = tokens.shape[0]
    wide_index = lax.axis_index(WIDE)
    feature_start = wide_index * local_width

    swap = [(0, 1), (1, 0)]
    chip_gate = jnp.concatenate([gate_up, lax.ppermute(gate_up, "core", swap)], axis=1)
    chip_down = jnp.concatenate([down_weight, lax.ppermute(down_weight, "core", swap)], axis=0)

    normed = rms_scale(tokens, attn_gain)
    shard_rows = gather_wide(normed, chips).reshape(SPAN, D)
    block_len = key_cache.shape[1]
    key_heads = jnp.transpose(key_cache[0].reshape(block_len, HEADS, HD), (1, 0, 2))
    value_heads = jnp.pad(
        jnp.transpose(value_cache[0].reshape(block_len, HEADS, HD), (1, 0, 2)),
        ((0, 0), (0, 0), (0, 4)),
    )
    shard_rows, key_heads, value_heads = lax.optimization_barrier((shard_rows, key_heads, value_heads))
    base_part = lax.optimization_barrier(
        jnp.dot(shard_rows, qkv_weight.reshape(D, 3 * local_width), preferred_element_type=jnp.float32)
    )
    sliced = lax.dynamic_slice_in_dim(shard_rows, feature_start, local_width, 1)
    partial_low = jnp.dot(sliced, adapter_down, preferred_element_type=jnp.float32)
    low_parts = send_rows(partial_low, WIDE, wide_size)
    own_low = jnp.sum(low_parts, axis=0).astype(jnp.bfloat16)
    lowrank = gather_rows(own_low, WIDE, wide_size).reshape(SPAN, 3, RANK)
    adapted = jnp.einsum("tcr,crd->tcd", lowrank, adapter_up, preferred_element_type=jnp.float32)
    projected = (base_part.reshape(SPAN, 3, local_width) + adapted).astype(jnp.bfloat16)
    query_own = projected[:, 0]
    new_keys = projected[:, 1]
    new_values = projected[:, 2]

    query_heads = gather_wide(query_own, chips).reshape(HEADS, SPAN, HD)
    block_start = wide_index * block_len
    length = cache_lengths[0]
    usable = (block_start + jnp.arange(block_len) < length) & (slot_mask[0] == 1)


    def cache_block(unused):
        scores = (
            jnp.einsum("hqd,hkd->hqk", query_heads, key_heads, preferred_element_type=jnp.float32)
            * score_scale
        )
        scores = jnp.where(usable, scores, NEG_LARGE)
        highest = jnp.max(scores, axis=-1)
        high, low = split_pair(highest)
        reference_max = high + low
        weights = jnp.where(usable, jnp.exp(scores - reference_max[..., None]), 0.0)
        totals = jnp.sum(weights, axis=-1)
        numerator = jnp.einsum(
            "hqk,hkd->hqd",
            weights.astype(jnp.bfloat16),
            value_heads,
            preferred_element_type=jnp.float32,
        )
        total_high, total_low = split_pair(totals)
        stats = jnp.stack([high, low, total_high, total_low], axis=-1).astype(jnp.bfloat16)
        return lax.dynamic_update_slice(numerator.astype(jnp.bfloat16), stats, (0, 0, HD))

    def skipped(unused):
        stats = jnp.zeros((HEADS, SPAN, 4), jnp.bfloat16).at[..., 0].set(NEG_LARGE)
        return jnp.concatenate([jnp.zeros((HEADS, SPAN, HD), jnp.bfloat16), stats], axis=-1)

    packed = lax.cond(block_start < length, cache_block, skipped, 0)
    parts = lax.all_to_all(packed, WIDE, 0, 0, tiled=True)
    part_num = parts[..., :HD].astype(jnp.float32)
    part_max = join_pair(parts[..., HD], parts[..., HD + 1])
    part_sum = join_pair(parts[..., HD + 2], parts[..., HD + 3])

    span_count = span_counts[0]
    query_pos = jnp.arange(SPAN)[:, None]
    key_pos = jnp.arange(SPAN)[None, :]
    span_ok = ((key_pos <= query_pos) & ((key_pos < span_count) | (key_pos == query_pos)))[
        :, None, :
    ]
    own_query = query_own.reshape(SPAN, local_heads, HD)
    own_keys = new_keys.reshape(SPAN, local_heads, HD)
    own_values = new_values.reshape(SPAN, local_heads, HD)
    own_scores = (
        jnp.einsum("qhd,khd->qhk", own_query, own_keys, preferred_element_type=jnp.float32)
        * score_scale
    )
    own_scores = jnp.where(span_ok, own_scores, NEG_LARGE)
    own_max = jnp.max(own_scores, axis=-1)
    own_weights = jnp.where(span_ok, jnp.exp(own_scores - own_max[..., None]), 0.0)
    own_sum = jnp.sum(own_weights, axis=-1)
    own_num = jnp.einsum(
        "qhk,khd->qhd",
        own_weights.astype(jnp.bfloat16),
        own_values,
        preferred_element_type=jnp.float32,
    )
    own_num = own_num.reshape(SPAN, HD)
    own_max = own_max.reshape(SPAN)
    own_sum = own_sum.reshape(SPAN)

    highest = jnp.maximum(jnp.max(part_max, axis=0), own_max)
    part_factor = jnp.exp(part_max - highest)
    own_factor = jnp.exp(own_max - highest)
    numerator = jnp.sum(part_num * part_factor[..., None], axis=0) + own_num * own_factor[:, None]
    totals = jnp.sum(part_sum * part_factor, axis=0) + own_sum * own_factor
    attention = (numerator / totals[:, None]).astype(jnp.bfloat16)

    head_out = jnp.dot(attention, out_weight, preferred_element_type=jnp.float32)
    out_parts = send_rows(head_out.astype(jnp.bfloat16), WIDE, wide_size)
    attn_out = jnp.sum(out_parts.astype(jnp.float32), axis=0)
    normed_mid = rms_scale(attn_out, mlp_gain)
    half_rows = gather_rows(normed_mid, HALF, half_size).reshape(half_size * own_rows, -1)
    both = jnp.einsum("td,cfd->ctf", half_rows, chip_gate, preferred_element_type=jnp.float32)
    hidden = (jax.nn.silu(both[0]) * both[1]).astype(jnp.bfloat16)
    ffn_part = jnp.dot(hidden, chip_down, preferred_element_type=jnp.float32)
    ffn_parts = send_rows(ffn_part.astype(jnp.bfloat16), HALF, half_size)
    hidden_out = jnp.sum(ffn_parts.astype(jnp.float32), axis=0).astype(jnp.bfloat16)
    return (hidden_out, attention, new_keys, new_values)


def solution(mesh):
    chips = mesh.shape["wide"] // 2
    split_mesh = jax.sharding.Mesh(
        mesh.devices.reshape(mesh.shape["req"], chips, 2), ("req", "chip", "core")
    )
    return jax.shard_map(
        body,
        mesh=split_mesh,
        in_specs=(
            P(("req",) + WIDE, None),
            P(),
            P(None, None, WIDE),
            P(WIDE, None),
            P(None, None, WIDE),
            P(WIDE, None),
            P(),
            P(None, ("req",) + WIDE, None),
            P(("req",) + WIDE, None),
            P("req", WIDE, None),
            P("req", WIDE, None),
            P("req"),
            P("req", WIDE),
            P("req"),
        ),
        out_specs=(P(("req",) + WIDE, None), P("req", WIDE), P("req", WIDE), P("req", WIDE)),
        check_vma=False,
    )
```

```python
import jax
import jax.numpy as jnp
from jax import lax
from jax.sharding import PartitionSpec as P

D = 7168
HEADS = 32
HD = 224
RANK = 128
SPAN = 128


EPSILON = 1e-05
NEG_LARGE = -1e30
WIDE = ("chip", "core")
HALF = ("req", "chip")


def rms_scale(values, gains):
    widened = values.astype(jnp.float32)
    meansq = jnp.mean(widened * widened, axis=-1, keepdims=True)
    return (widened * lax.rsqrt(meansq + EPSILON) * gains.astype(jnp.float32)).astype(jnp.bfloat16)


def gather_rows(piece, axis, count):
    spread = jnp.broadcast_to(piece[None], (count,) + piece.shape)
    return lax.all_to_all(spread, axis, 0, 0, tiled=True)


def gather_wide(piece, chips, along_rows):
    own = gather_rows(piece, "chip", chips)
    other = lax.ppermute(own, "core", [(0, 1), (1, 0)])
    core = lax.axis_index("core")
    if along_rows:
        rows = piece.shape[0]
        joined = jnp.zeros((chips, 2 * rows) + piece.shape[1:], piece.dtype)
        own_at, other_at = core * rows, (1 - core) * rows
    else:
        own, other = own[:, None], other[:, None]
        joined = jnp.zeros((chips, 2) + piece.shape, piece.dtype)
        own_at, other_at = core, 1 - core
    joined = lax.dynamic_update_slice_in_dim(joined, own, own_at, axis=1)
    joined = lax.dynamic_update_slice_in_dim(joined, other, other_at, axis=1)
    return joined.reshape((2 * chips,) + piece.shape)


def send_rows(values, axis, count):
    blocks = values.reshape((count, values.shape[0] // count) + values.shape[1:])
    return lax.all_to_all(blocks, axis, 0, 0, tiled=True)


def split_pair(values):
    high = lax.reduce_precision(values, exponent_bits=8, mantissa_bits=7)
    low = lax.reduce_precision(values - high, exponent_bits=8, mantissa_bits=7)
    return high, low


def join_pair(high, low):
    return high.astype(jnp.float32) + low.astype(jnp.float32)


def body(
    tokens,
    attn_gain,
    qkv_weight,
    adapter_down,
    adapter_up,
    out_weight,
    mlp_gain,
    gate_up,
    down_weight,
    key_cache,
    value_cache,
    cache_lengths,
    slot_mask,
    span_counts,
):
    score_scale = HD ** (-0.5)
    wide_size = lax.psum(1, WIDE)
    half_size = lax.psum(1, HALF)
    chips = lax.psum(1, "chip")
    local_width = qkv_weight.shape[2]
    local_heads = local_width // HD
    own_rows = tokens.shape[0]
    wide_index = lax.axis_index(WIDE)
    feature_start = wide_index * local_width

    swap = [(0, 1), (1, 0)]
    chip_gate = jnp.concatenate([gate_up, lax.ppermute(gate_up, "core", swap)], axis=1)
    chip_down = jnp.concatenate([down_weight, lax.ppermute(down_weight, "core", swap)], axis=0)

    normed = rms_scale(tokens, attn_gain)
    shard_rows = gather_wide(normed, chips, True).reshape(SPAN, D)
    block_len = key_cache.shape[1]
    key_heads = jnp.transpose(key_cache[0].reshape(block_len, HEADS, HD), (1, 0, 2))
    value_heads = jnp.pad(
        jnp.transpose(value_cache[0].reshape(block_len, HEADS, HD), (1, 0, 2)),
        ((0, 0), (0, 0), (0, 4)),
    )
    shard_rows, key_heads, value_heads = lax.optimization_barrier((shard_rows, key_heads, value_heads))
    base_part = lax.optimization_barrier(
        jnp.dot(shard_rows, qkv_weight.reshape(D, 3 * local_width), preferred_element_type=jnp.float32)
    )
    sliced = lax.dynamic_slice_in_dim(shard_rows, feature_start, local_width, 1)
    partial_low = jnp.dot(sliced, adapter_down, preferred_element_type=jnp.float32)
    low_parts = send_rows(partial_low, WIDE, wide_size)
    own_low = jnp.sum(low_parts, axis=0).astype(jnp.bfloat16)
    lowrank = gather_rows(own_low, WIDE, wide_size).reshape(SPAN, 3, RANK)
    adapted = jnp.einsum("tcr,crd->tcd", lowrank, adapter_up, preferred_element_type=jnp.float32)
    projected = (base_part.reshape(SPAN, 3, local_width) + adapted).astype(jnp.bfloat16)
    query_own = projected[:, 0]
    new_keys = projected[:, 1]
    new_values = projected[:, 2]

    query_heads = gather_wide(query_own, chips, False).reshape(HEADS, SPAN, HD)
    block_start = wide_index * block_len
    length = cache_lengths[0]
    usable = (block_start + jnp.arange(block_len) < length) & (slot_mask[0] == 1)


    def cache_block(unused):
        scores = (
            jnp.einsum("hqd,hkd->hqk", query_heads, key_heads, preferred_element_type=jnp.float32)
            * score_scale
        )
        scores = jnp.where(usable, scores, NEG_LARGE)
        highest = jnp.max(scores, axis=-1)
        high, low = split_pair(highest)
        reference_max = high + low
        weights = jnp.where(usable, jnp.exp(scores - reference_max[..., None]), 0.0)
        totals = jnp.sum(weights, axis=-1)
        numerator = jnp.einsum(
            "hqk,hkd->hqd",
            weights.astype(jnp.bfloat16),
            value_heads,
            preferred_element_type=jnp.float32,
        )
        total_high, total_low = split_pair(totals)
        stats = jnp.stack([high, low, total_high, total_low], axis=-1).astype(jnp.bfloat16)
        return lax.dynamic_update_slice(numerator.astype(jnp.bfloat16), stats, (0, 0, HD))

    def skipped(unused):
        stats = jnp.zeros((HEADS, SPAN, 4), jnp.bfloat16).at[..., 0].set(NEG_LARGE)
        return jnp.concatenate([jnp.zeros((HEADS, SPAN, HD), jnp.bfloat16), stats], axis=-1)

    packed = lax.cond(block_start < length, cache_block, skipped, 0)
    parts = lax.all_to_all(packed, WIDE, 0, 0, tiled=True)
    part_num = parts[..., :HD].astype(jnp.float32)
    part_max = join_pair(parts[..., HD], parts[..., HD + 1])
    part_sum = join_pair(parts[..., HD + 2], parts[..., HD + 3])

    span_count = span_counts[0]
    query_pos = jnp.arange(SPAN)[:, None]
    key_pos = jnp.arange(SPAN)[None, :]
    span_ok = ((key_pos <= query_pos) & ((key_pos < span_count) | (key_pos == query_pos)))[
        :, None, :
    ]
    own_query = query_own.reshape(SPAN, local_heads, HD)
    own_keys = new_keys.reshape(SPAN, local_heads, HD)
    own_values = new_values.reshape(SPAN, local_heads, HD)
    own_scores = (
        jnp.einsum("qhd,khd->qhk", own_query, own_keys, preferred_element_type=jnp.float32)
        * score_scale
    )
    own_scores = jnp.where(span_ok, own_scores, NEG_LARGE)
    own_max = jnp.max(own_scores, axis=-1)
    own_weights = jnp.where(span_ok, jnp.exp(own_scores - own_max[..., None]), 0.0)
    own_sum = jnp.sum(own_weights, axis=-1)
    own_num = jnp.einsum(
        "qhk,khd->qhd",
        own_weights.astype(jnp.bfloat16),
        own_values,
        preferred_element_type=jnp.float32,
    )
    own_num = own_num.reshape(SPAN, HD)
    own_max = own_max.reshape(SPAN)
    own_sum = own_sum.reshape(SPAN)

    highest = jnp.maximum(jnp.max(part_max, axis=0), own_max)
    part_factor = jnp.exp(part_max - highest)
    own_factor = jnp.exp(own_max - highest)
    numerator = jnp.sum(part_num * part_factor[..., None], axis=0) + own_num * own_factor[:, None]
    totals = jnp.sum(part_sum * part_factor, axis=0) + own_sum * own_factor
    attention = (numerator / totals[:, None]).astype(jnp.bfloat16)

    head_out = jnp.dot(attention, out_weight, preferred_element_type=jnp.float32)
    out_parts = send_rows(head_out.astype(jnp.bfloat16), WIDE, wide_size)
    attn_out = jnp.sum(out_parts.astype(jnp.float32), axis=0)
    normed_mid = rms_scale(attn_out, mlp_gain)
    half_rows = gather_rows(normed_mid, HALF, half_size)
    both = jnp.einsum("gtd,cfd->cgtf", half_rows, chip_gate, preferred_element_type=jnp.float32)
    hidden = (jax.nn.silu(both[0]) * both[1]).astype(jnp.bfloat16)
    ffn_part = jnp.einsum("gtf,fd->gtd", hidden, chip_down, preferred_element_type=jnp.float32)
    ffn_parts = lax.all_to_all(ffn_part.astype(jnp.bfloat16), HALF, 0, 0, tiled=True)
    hidden_out = jnp.sum(ffn_parts.astype(jnp.float32), axis=0).astype(jnp.bfloat16)
    return (hidden_out, attention, new_keys, new_values)


def solution(mesh):
    chips = mesh.shape["wide"] // 2
    split_mesh = jax.sharding.Mesh(
        mesh.devices.reshape(mesh.shape["req"], chips, 2), ("req", "chip", "core")
    )
    return jax.shard_map(
        body,
        mesh=split_mesh,
        in_specs=(
            P(("req",) + WIDE, None),
            P(),
            P(None, None, WIDE),
            P(WIDE, None),
            P(None, None, WIDE),
            P(WIDE, None),
            P(),
            P(None, ("req",) + WIDE, None),
            P(("req",) + WIDE, None),
            P("req", WIDE, None),
            P("req", WIDE, None),
            P("req"),
            P("req", WIDE),
            P("req"),
        ),
        out_specs=(P(("req",) + WIDE, None), P("req", WIDE), P("req", WIDE), P("req", WIDE)),
        check_vma=False,
    )
```

```python
import jax
import jax.numpy as jnp
from jax import lax
from jax.sharding import PartitionSpec as P

D = 7168
HEADS = 32
HD = 224
RANK = 128
SPAN = 128


EPSILON = 1e-05
NEG_LARGE = -1e30
WIDE = ("chip", "core")
HALF = ("req", "chip")


def rms_scale(values, gains):
    widened = values.astype(jnp.float32)
    meansq = jnp.mean(widened * widened, axis=-1, keepdims=True)
    return (widened * lax.rsqrt(meansq + EPSILON) * gains.astype(jnp.float32)).astype(jnp.bfloat16)


def gather_rows(piece, axis, count):
    spread = jnp.broadcast_to(piece[None], (count,) + piece.shape)
    return lax.all_to_all(spread, axis, 0, 0, tiled=True)


def gather_wide(piece, chips):
    own = gather_rows(piece, "chip", chips)[:, None]
    other = lax.ppermute(own, "core", [(0, 1), (1, 0)])
    core = lax.axis_index("core")
    joined = jnp.zeros((chips, 2) + piece.shape, piece.dtype)
    joined = lax.dynamic_update_slice_in_dim(joined, own, core, axis=1)
    joined = lax.dynamic_update_slice_in_dim(joined, other, 1 - core, axis=1)
    return joined.reshape((2 * chips,) + piece.shape)


def send_rows(values, axis, count):
    blocks = values.reshape((count, values.shape[0] // count) + values.shape[1:])
    return lax.all_to_all(blocks, axis, 0, 0, tiled=True)


def split_pair(values):
    high = lax.reduce_precision(values, exponent_bits=8, mantissa_bits=7)
    low = lax.reduce_precision(values - high, exponent_bits=8, mantissa_bits=7)
    return high, low


def join_pair(high, low):
    return high.astype(jnp.float32) + low.astype(jnp.float32)


def body(
    tokens,
    attn_gain,
    qkv_weight,
    adapter_down,
    adapter_up,
    out_weight,
    mlp_gain,
    gate_up,
    down_weight,
    key_cache,
    value_cache,
    cache_lengths,
    slot_mask,
    span_counts,
):
    score_scale = HD ** (-0.5)
    wide_size = lax.psum(1, WIDE)
    half_size = lax.psum(1, HALF)
    chips = lax.psum(1, "chip")
    local_width = qkv_weight.shape[2]
    local_heads = local_width // HD
    own_rows = tokens.shape[0]
    wide_index = lax.axis_index(WIDE)
    feature_start = wide_index * local_width

    swap = [(0, 1), (1, 0)]
    chip_gate = jnp.concatenate([gate_up, lax.ppermute(gate_up, "core", swap)], axis=1)
    chip_down = jnp.concatenate([down_weight, lax.ppermute(down_weight, "core", swap)], axis=0)

    normed = rms_scale(tokens, attn_gain)
    shard_rows = gather_wide(normed, chips).reshape(SPAN, D)
    block_len = key_cache.shape[1]
    key_heads = jnp.transpose(key_cache[0].reshape(block_len, HEADS, HD), (1, 0, 2))
    value_heads = jnp.pad(
        jnp.transpose(value_cache[0].reshape(block_len, HEADS, HD), (1, 0, 2)),
        ((0, 0), (0, 0), (0, 4)),
    )
    shard_rows, key_heads, value_heads = lax.optimization_barrier((shard_rows, key_heads, value_heads))
    base_part = lax.optimization_barrier(
        jnp.dot(shard_rows, qkv_weight.reshape(D, 3 * local_width), preferred_element_type=jnp.float32)
    )
    sliced = lax.dynamic_slice_in_dim(shard_rows, feature_start, local_width, 1)
    partial_low = jnp.dot(sliced, adapter_down, preferred_element_type=jnp.float32)
    low_parts = send_rows(partial_low, WIDE, wide_size)
    own_low = jnp.sum(low_parts, axis=0).astype(jnp.bfloat16)
    lowrank = gather_rows(own_low, WIDE, wide_size).reshape(SPAN, 3, RANK)
    adapted = jnp.einsum("tcr,crd->tcd", lowrank, adapter_up, preferred_element_type=jnp.float32)
    projected = (base_part.reshape(SPAN, 3, local_width) + adapted).astype(jnp.bfloat16)
    query_own = projected[:, 0]
    new_keys = projected[:, 1]
    new_values = projected[:, 2]

    query_heads = gather_wide(query_own, chips).reshape(HEADS, SPAN, HD)
    block_start = wide_index * block_len
    length = cache_lengths[0]
    usable = (block_start + jnp.arange(block_len) < length) & (slot_mask[0] == 1)


    def cache_block(unused):
        scores = (
            jnp.einsum("hqd,hkd->hqk", query_heads, key_heads, preferred_element_type=jnp.float32)
            * score_scale
        )
        scores = jnp.where(usable, scores, NEG_LARGE)
        highest = jnp.max(scores, axis=-1)
        high, low = split_pair(highest)
        reference_max = high + low
        weights = jnp.where(usable, jnp.exp(scores - reference_max[..., None]), 0.0)
        totals = jnp.sum(weights, axis=-1)
        numerator = jnp.einsum(
            "hqk,hkd->hqd",
            weights.astype(jnp.bfloat16),
            value_heads,
            preferred_element_type=jnp.float32,
        )
        total_high, total_low = split_pair(totals)
        stats = jnp.stack([high, low, total_high, total_low], axis=-1).astype(jnp.bfloat16)
        return lax.dynamic_update_slice(numerator.astype(jnp.bfloat16), stats, (0, 0, HD))

    def skipped(unused):
        stats = jnp.zeros((HEADS, SPAN, 4), jnp.bfloat16).at[..., 0].set(NEG_LARGE)
        return jnp.concatenate([jnp.zeros((HEADS, SPAN, HD), jnp.bfloat16), stats], axis=-1)

    packed = lax.cond(block_start < length, cache_block, skipped, 0)
    parts = lax.all_to_all(packed, WIDE, 0, 0, tiled=True)
    part_num = parts[..., :HD].astype(jnp.float32)
    part_max = join_pair(parts[..., HD], parts[..., HD + 1])
    part_sum = join_pair(parts[..., HD + 2], parts[..., HD + 3])

    span_count = span_counts[0]
    query_pos = jnp.arange(SPAN)[:, None]
    key_pos = jnp.arange(SPAN)[None, :]
    span_ok = ((key_pos <= query_pos) & ((key_pos < span_count) | (key_pos == query_pos)))[
        :, None, :
    ]
    own_query = query_own.reshape(SPAN, local_heads, HD)
    own_keys = new_keys.reshape(SPAN, local_heads, HD)
    own_values = new_values.reshape(SPAN, local_heads, HD)
    own_scores = (
        jnp.einsum("qhd,khd->qhk", own_query, own_keys, preferred_element_type=jnp.float32)
        * score_scale
    )
    own_scores = jnp.where(span_ok, own_scores, NEG_LARGE)
    own_max = jnp.max(own_scores, axis=-1)
    own_weights = jnp.where(span_ok, jnp.exp(own_scores - own_max[..., None]), 0.0)
    own_sum = jnp.sum(own_weights, axis=-1)
    own_num = jnp.einsum(
        "qhk,khd->qhd",
        own_weights.astype(jnp.bfloat16),
        own_values,
        preferred_element_type=jnp.float32,
    )
    own_num = own_num.reshape(SPAN, HD)
    own_max = own_max.reshape(SPAN)
    own_sum = own_sum.reshape(SPAN)

    highest = jnp.maximum(jnp.max(part_max, axis=0), own_max)
    part_factor = jnp.exp(part_max - highest)
    own_factor = jnp.exp(own_max - highest)
    numerator = jnp.sum(part_num * part_factor[..., None], axis=0) + own_num * own_factor[:, None]
    totals = jnp.sum(part_sum * part_factor, axis=0) + own_sum * own_factor
    attention = (numerator / totals[:, None]).astype(jnp.bfloat16)

    head_out = jnp.dot(attention, out_weight, preferred_element_type=jnp.float32)
    out_parts = send_rows(head_out.astype(jnp.bfloat16), WIDE, wide_size)
    attn_out = jnp.sum(out_parts.astype(jnp.float32), axis=0)
    normed_mid = rms_scale(attn_out, mlp_gain)
    half_rows = gather_rows(normed_mid, HALF, half_size)
    both = jnp.einsum("gtd,cfd->cgtf", half_rows, chip_gate, preferred_element_type=jnp.float32)
    hidden = (jax.nn.silu(both[0]) * both[1]).astype(jnp.bfloat16)
    ffn_part = jnp.einsum("gtf,fd->gtd", hidden, chip_down, preferred_element_type=jnp.float32)
    ffn_parts = lax.all_to_all(ffn_part.astype(jnp.bfloat16), HALF, 0, 0, tiled=True)
    hidden_out = jnp.sum(ffn_parts.astype(jnp.float32), axis=0).astype(jnp.bfloat16)
    return (hidden_out, attention, new_keys, new_values)


def solution(mesh):
    chips = mesh.shape["wide"] // 2
    split_mesh = jax.sharding.Mesh(
        mesh.devices.reshape(mesh.shape["req"], chips, 2), ("req", "chip", "core")
    )
    return jax.shard_map(
        body,
        mesh=split_mesh,
        in_specs=(
            P(("req",) + WIDE, None),
            P(),
            P(None, None, WIDE),
            P(WIDE, None),
            P(None, None, WIDE),
            P(WIDE, None),
            P(),
            P(None, ("req",) + WIDE, None),
            P(("req",) + WIDE, None),
            P("req", WIDE, None),
            P("req", WIDE, None),
            P("req"),
            P("req", WIDE),
            P("req"),
        ),
        out_specs=(P(("req",) + WIDE, None), P("req", WIDE), P("req", WIDE), P("req", WIDE)),
        check_vma=False,
    )
```

```python
import jax
import jax.numpy as jnp
from jax import lax
from jax.sharding import PartitionSpec as P

D = 7168
HEADS = 32
HD = 224
RANK = 128
SPAN = 128


EPSILON = 1e-05
NEG_LARGE = -1e30
WIDE = ("chip", "core")
HALF = ("req", "chip")


def rms_scale(values, gains):
    widened = values.astype(jnp.float32)
    meansq = jnp.mean(widened * widened, axis=-1, keepdims=True)
    return (widened * lax.rsqrt(meansq + EPSILON) * gains.astype(jnp.float32)).astype(jnp.bfloat16)


def gather_rows(piece, axis, count):
    spread = jnp.broadcast_to(piece[None], (count,) + piece.shape)
    return lax.all_to_all(spread, axis, 0, 0, tiled=True)


def gather_wide(piece, chips):
    own = gather_rows(piece, "chip", chips)[:, None]
    other = lax.ppermute(own, "core", [(0, 1), (1, 0)])
    core = lax.axis_index("core")
    joined = jnp.zeros((chips, 2) + piece.shape, piece.dtype)
    joined = lax.dynamic_update_slice_in_dim(joined, own, core, axis=1)
    joined = lax.dynamic_update_slice_in_dim(joined, other, 1 - core, axis=1)
    return joined.reshape((2 * chips,) + piece.shape)


def send_rows(values, axis, count):
    blocks = values.reshape((count, values.shape[0] // count) + values.shape[1:])
    return lax.all_to_all(blocks, axis, 0, 0, tiled=True)


def split_pair(values):
    high = lax.reduce_precision(values, exponent_bits=8, mantissa_bits=7)
    low = lax.reduce_precision(values - high, exponent_bits=8, mantissa_bits=7)
    return high, low


def join_pair(high, low):
    return high.astype(jnp.float32) + low.astype(jnp.float32)


def join_partials(first, second):
    first_max = join_pair(first[..., HD], first[..., HD + 1])
    second_max = join_pair(second[..., HD], second[..., HD + 1])
    highest = jnp.maximum(first_max, second_max)
    first_factor = jnp.exp(first_max - highest)
    second_factor = jnp.exp(second_max - highest)
    numerator = (
        first[..., :HD].astype(jnp.float32) * first_factor[..., None]
        + second[..., :HD].astype(jnp.float32) * second_factor[..., None]
    )
    totals = join_pair(first[..., HD + 2], first[..., HD + 3]) * first_factor + join_pair(
        second[..., HD + 2], second[..., HD + 3]
    ) * second_factor
    high, low = split_pair(highest)
    shift = jnp.exp(highest - (high + low))
    total_high, total_low = split_pair(totals * shift)
    stats = jnp.stack([high, low, total_high, total_low], axis=-1).astype(jnp.bfloat16)
    return jnp.concatenate([(numerator * shift[..., None]).astype(jnp.bfloat16), stats], axis=-1)


def body(
    tokens,
    attn_gain,
    qkv_weight,
    adapter_down,
    adapter_up,
    out_weight,
    mlp_gain,
    gate_up,
    down_weight,
    key_cache,
    value_cache,
    cache_lengths,
    slot_mask,
    span_counts,
):
    score_scale = HD ** (-0.5)
    wide_size = lax.psum(1, WIDE)
    half_size = lax.psum(1, HALF)
    chips = lax.psum(1, "chip")
    local_width = qkv_weight.shape[2]
    local_heads = local_width // HD
    own_rows = tokens.shape[0]
    wide_index = lax.axis_index(WIDE)
    feature_start = wide_index * local_width

    swap = [(0, 1), (1, 0)]
    chip_gate = jnp.concatenate([gate_up, lax.ppermute(gate_up, "core", swap)], axis=1)
    chip_down = jnp.concatenate([down_weight, lax.ppermute(down_weight, "core", swap)], axis=0)

    normed = rms_scale(tokens, attn_gain)
    shard_rows = gather_wide(normed, chips).reshape(SPAN, D)
    block_len = key_cache.shape[1]
    key_heads = jnp.transpose(key_cache[0].reshape(block_len, HEADS, HD), (1, 0, 2))
    value_heads = jnp.pad(
        jnp.transpose(value_cache[0].reshape(block_len, HEADS, HD), (1, 0, 2)),
        ((0, 0), (0, 0), (0, 4)),
    )
    shard_rows, key_heads, value_heads = lax.optimization_barrier((shard_rows, key_heads, value_heads))
    base_part = lax.optimization_barrier(
        jnp.dot(shard_rows, qkv_weight.reshape(D, 3 * local_width), preferred_element_type=jnp.float32)
    )
    sliced = lax.dynamic_slice_in_dim(shard_rows, feature_start, local_width, 1)
    partial_low = jnp.dot(sliced, adapter_down, preferred_element_type=jnp.float32)
    low_parts = send_rows(partial_low, WIDE, wide_size)
    own_low = jnp.sum(low_parts, axis=0).astype(jnp.bfloat16)
    lowrank = gather_rows(own_low, WIDE, wide_size).reshape(SPAN, 3, RANK)
    adapted = jnp.einsum("tcr,crd->tcd", lowrank, adapter_up, preferred_element_type=jnp.float32)
    projected = (base_part.reshape(SPAN, 3, local_width) + adapted).astype(jnp.bfloat16)
    query_own = projected[:, 0]
    new_keys = projected[:, 1]
    new_values = projected[:, 2]

    query_heads = gather_wide(query_own, chips).reshape(HEADS, SPAN, HD)
    block_start = wide_index * block_len
    length = cache_lengths[0]
    usable = (block_start + jnp.arange(block_len) < length) & (slot_mask[0] == 1)


    def cache_block(unused):
        scores = (
            jnp.einsum("hqd,hkd->hqk", query_heads, key_heads, preferred_element_type=jnp.float32)
            * score_scale
        )
        scores = jnp.where(usable, scores, NEG_LARGE)
        highest = jnp.max(scores, axis=-1)
        high, low = split_pair(highest)
        reference_max = high + low
        weights = jnp.where(usable, jnp.exp(scores - reference_max[..., None]), 0.0)
        totals = jnp.sum(weights, axis=-1)
        numerator = jnp.einsum(
            "hqk,hkd->hqd",
            weights.astype(jnp.bfloat16),
            value_heads,
            preferred_element_type=jnp.float32,
        )
        total_high, total_low = split_pair(totals)
        stats = jnp.stack([high, low, total_high, total_low], axis=-1).astype(jnp.bfloat16)
        return lax.dynamic_update_slice(numerator.astype(jnp.bfloat16), stats, (0, 0, HD))

    def skipped(unused):
        stats = jnp.zeros((HEADS, SPAN, 4), jnp.bfloat16).at[..., 0].set(NEG_LARGE)
        return jnp.concatenate([jnp.zeros((HEADS, SPAN, HD), jnp.bfloat16), stats], axis=-1)

    packed = lax.cond(block_start < length, cache_block, skipped, 0)
    core = lax.axis_index("core")
    by_side = packed.reshape(HEADS // 2, 2, SPAN, HD + 4)
    kept = lax.dynamic_index_in_dim(by_side, core, axis=1, keepdims=False)
    given = lax.dynamic_index_in_dim(by_side, 1 - core, axis=1, keepdims=False)
    taken = lax.ppermute(given, "core", [(0, 1), (1, 0)])
    joined = join_partials(kept, taken)
    parts = lax.all_to_all(joined, "chip", 0, 0, tiled=True)
    part_num = parts[..., :HD].astype(jnp.float32)
    part_max = join_pair(parts[..., HD], parts[..., HD + 1])
    part_sum = join_pair(parts[..., HD + 2], parts[..., HD + 3])

    span_count = span_counts[0]
    query_pos = jnp.arange(SPAN)[:, None]
    key_pos = jnp.arange(SPAN)[None, :]
    span_ok = ((key_pos <= query_pos) & ((key_pos < span_count) | (key_pos == query_pos)))[
        :, None, :
    ]
    own_query = query_own.reshape(SPAN, local_heads, HD)
    own_keys = new_keys.reshape(SPAN, local_heads, HD)
    own_values = new_values.reshape(SPAN, local_heads, HD)
    own_scores = (
        jnp.einsum("qhd,khd->qhk", own_query, own_keys, preferred_element_type=jnp.float32)
        * score_scale
    )
    own_scores = jnp.where(span_ok, own_scores, NEG_LARGE)
    own_max = jnp.max(own_scores, axis=-1)
    own_weights = jnp.where(span_ok, jnp.exp(own_scores - own_max[..., None]), 0.0)
    own_sum = jnp.sum(own_weights, axis=-1)
    own_num = jnp.einsum(
        "qhk,khd->qhd",
        own_weights.astype(jnp.bfloat16),
        own_values,
        preferred_element_type=jnp.float32,
    )
    own_num = own_num.reshape(SPAN, HD)
    own_max = own_max.reshape(SPAN)
    own_sum = own_sum.reshape(SPAN)

    highest = jnp.maximum(jnp.max(part_max, axis=0), own_max)
    part_factor = jnp.exp(part_max - highest)
    own_factor = jnp.exp(own_max - highest)
    numerator = jnp.sum(part_num * part_factor[..., None], axis=0) + own_num * own_factor[:, None]
    totals = jnp.sum(part_sum * part_factor, axis=0) + own_sum * own_factor
    attention = (numerator / totals[:, None]).astype(jnp.bfloat16)

    head_out = jnp.dot(attention, out_weight, preferred_element_type=jnp.float32)
    out_parts = send_rows(head_out.astype(jnp.bfloat16), WIDE, wide_size)
    attn_out = jnp.sum(out_parts.astype(jnp.float32), axis=0)
    normed_mid = rms_scale(attn_out, mlp_gain)
    half_rows = gather_rows(normed_mid, HALF, half_size)
    both = jnp.einsum("gtd,cfd->cgtf", half_rows, chip_gate, preferred_element_type=jnp.float32)
    hidden = (jax.nn.silu(both[0]) * both[1]).astype(jnp.bfloat16)
    ffn_part = jnp.einsum("gtf,fd->gtd", hidden, chip_down, preferred_element_type=jnp.float32)
    ffn_parts = lax.all_to_all(ffn_part.astype(jnp.bfloat16), HALF, 0, 0, tiled=True)
    hidden_out = jnp.sum(ffn_parts.astype(jnp.float32), axis=0).astype(jnp.bfloat16)
    return (hidden_out, attention, new_keys, new_values)


def solution(mesh):
    chips = mesh.shape["wide"] // 2
    split_mesh = jax.sharding.Mesh(
        mesh.devices.reshape(mesh.shape["req"], chips, 2), ("req", "chip", "core")
    )
    return jax.shard_map(
        body,
        mesh=split_mesh,
        in_specs=(
            P(("req",) + WIDE, None),
            P(),
            P(None, None, WIDE),
            P(WIDE, None),
            P(None, None, WIDE),
            P(WIDE, None),
            P(),
            P(None, ("req",) + WIDE, None),
            P(("req",) + WIDE, None),
            P("req", WIDE, None),
            P("req", WIDE, None),
            P("req"),
            P("req", WIDE),
            P("req"),
        ),
        out_specs=(P(("req",) + WIDE, None), P("req", WIDE), P("req", WIDE), P("req", WIDE)),
        check_vma=False,
    )
```

```python
import jax
import jax.numpy as jnp
from jax import lax
from jax.sharding import PartitionSpec as P

D = 7168
HEADS = 32
HD = 224
RANK = 128
SPAN = 128


EPSILON = 1e-05
NEG_LARGE = -1e30
WIDE = ("chip", "core")
HALF = ("req", "chip")


def rms_scale(values, gains):
    widened = values.astype(jnp.float32)
    meansq = jnp.mean(widened * widened, axis=-1, keepdims=True)
    return (widened * lax.rsqrt(meansq + EPSILON) * gains.astype(jnp.float32)).astype(jnp.bfloat16)


def gather_rows(piece, axis, count):
    spread = jnp.broadcast_to(piece[None], (count,) + piece.shape)
    return lax.all_to_all(spread, axis, 0, 0, tiled=True)


def gather_wide(piece, chips):
    own = gather_rows(piece, "chip", chips)[:, None]
    other = lax.ppermute(own, "core", [(0, 1), (1, 0)])
    core = lax.axis_index("core")
    joined = jnp.zeros((chips, 2) + piece.shape, piece.dtype)
    joined = lax.dynamic_update_slice_in_dim(joined, own, core, axis=1)
    joined = lax.dynamic_update_slice_in_dim(joined, other, 1 - core, axis=1)
    return joined.reshape((2 * chips,) + piece.shape)


def send_rows(values, axis, count):
    blocks = values.reshape((count, values.shape[0] // count) + values.shape[1:])
    return lax.all_to_all(blocks, axis, 0, 0, tiled=True)


def split_pair(values):
    high = lax.reduce_precision(values, exponent_bits=8, mantissa_bits=7)
    low = lax.reduce_precision(values - high, exponent_bits=8, mantissa_bits=7)
    return high, low


def join_pair(high, low):
    return high.astype(jnp.float32) + low.astype(jnp.float32)


def join_partials(first, second):
    first_max = join_pair(first[..., HD], first[..., HD + 1])
    second_max = join_pair(second[..., HD], second[..., HD + 1])
    highest = jnp.maximum(first_max, second_max)
    first_factor = jnp.exp(first_max - highest)
    second_factor = jnp.exp(second_max - highest)
    numerator = (
        first[..., :HD].astype(jnp.float32) * first_factor[..., None]
        + second[..., :HD].astype(jnp.float32) * second_factor[..., None]
    )
    totals = join_pair(first[..., HD + 2], first[..., HD + 3]) * first_factor + join_pair(
        second[..., HD + 2], second[..., HD + 3]
    ) * second_factor
    high, low = split_pair(highest)
    shift = jnp.exp(highest - (high + low))
    total_high, total_low = split_pair(totals * shift)
    stats = jnp.stack([high, low, total_high, total_low], axis=-1).astype(jnp.bfloat16)
    return jnp.concatenate([(numerator * shift[..., None]).astype(jnp.bfloat16), stats], axis=-1)


def body(
    tokens,
    attn_gain,
    qkv_weight,
    adapter_down,
    adapter_up,
    out_weight,
    mlp_gain,
    gate_up,
    down_weight,
    key_cache,
    value_cache,
    cache_lengths,
    slot_mask,
    span_counts,
):
    score_scale = HD ** (-0.5)
    wide_size = lax.psum(1, WIDE)
    half_size = lax.psum(1, HALF)
    chips = lax.psum(1, "chip")
    local_width = qkv_weight.shape[2]
    local_heads = local_width // HD
    own_rows = tokens.shape[0]
    wide_index = lax.axis_index(WIDE)
    feature_start = wide_index * local_width

    swap = [(0, 1), (1, 0)]
    chip_gate = jnp.concatenate([gate_up, lax.ppermute(gate_up, "core", swap)], axis=1)
    chip_down = jnp.concatenate([down_weight, lax.ppermute(down_weight, "core", swap)], axis=0)

    normed = rms_scale(tokens, attn_gain)
    shard_rows = gather_wide(normed, chips).reshape(SPAN, D)
    block_len = key_cache.shape[1]
    key_heads = jnp.transpose(key_cache[0].reshape(block_len, HEADS, HD), (1, 0, 2))
    value_heads = jnp.pad(
        jnp.transpose(value_cache[0].reshape(block_len, HEADS, HD), (1, 0, 2)),
        ((0, 0), (0, 0), (0, 4)),
    )
    shard_rows, key_heads, value_heads = lax.optimization_barrier((shard_rows, key_heads, value_heads))
    base_part = lax.optimization_barrier(
        jnp.dot(shard_rows, qkv_weight.reshape(D, 3 * local_width), preferred_element_type=jnp.float32)
    )
    sliced = lax.dynamic_slice_in_dim(shard_rows, feature_start, local_width, 1)
    partial_low = jnp.dot(sliced, adapter_down, preferred_element_type=jnp.float32)
    low_core = lax.axis_index("core")
    low_sides = partial_low.reshape(chips, 2, own_rows, 3 * RANK)
    low_kept = lax.dynamic_index_in_dim(low_sides, low_core, axis=1, keepdims=False)
    low_given = lax.dynamic_index_in_dim(low_sides, 1 - low_core, axis=1, keepdims=False)
    low_chip = low_kept + lax.ppermute(low_given, "core", [(0, 1), (1, 0)])
    low_parts = lax.all_to_all(low_chip, "chip", 0, 0, tiled=True)
    own_low = jnp.sum(low_parts, axis=0).astype(jnp.bfloat16)
    lowrank = gather_rows(own_low, WIDE, wide_size).reshape(SPAN, 3, RANK)
    adapted = jnp.einsum("tcr,crd->tcd", lowrank, adapter_up, preferred_element_type=jnp.float32)
    projected = (base_part.reshape(SPAN, 3, local_width) + adapted).astype(jnp.bfloat16)
    query_own = projected[:, 0]
    new_keys = projected[:, 1]
    new_values = projected[:, 2]

    query_heads = gather_wide(query_own, chips).reshape(HEADS, SPAN, HD)
    block_start = wide_index * block_len
    length = cache_lengths[0]
    usable = (block_start + jnp.arange(block_len) < length) & (slot_mask[0] == 1)


    def cache_block(unused):
        scores = (
            jnp.einsum("hqd,hkd->hqk", query_heads, key_heads, preferred_element_type=jnp.float32)
            * score_scale
        )
        scores = jnp.where(usable, scores, NEG_LARGE)
        highest = jnp.max(scores, axis=-1)
        high, low = split_pair(highest)
        reference_max = high + low
        weights = jnp.where(usable, jnp.exp(scores - reference_max[..., None]), 0.0)
        totals = jnp.sum(weights, axis=-1)
        numerator = jnp.einsum(
            "hqk,hkd->hqd",
            weights.astype(jnp.bfloat16),
            value_heads,
            preferred_element_type=jnp.float32,
        )
        total_high, total_low = split_pair(totals)
        stats = jnp.stack([high, low, total_high, total_low], axis=-1).astype(jnp.bfloat16)
        return lax.dynamic_update_slice(numerator.astype(jnp.bfloat16), stats, (0, 0, HD))

    def skipped(unused):
        stats = jnp.zeros((HEADS, SPAN, 4), jnp.bfloat16).at[..., 0].set(NEG_LARGE)
        return jnp.concatenate([jnp.zeros((HEADS, SPAN, HD), jnp.bfloat16), stats], axis=-1)

    packed = lax.cond(block_start < length, cache_block, skipped, 0)
    core = lax.axis_index("core")
    by_side = packed.reshape(HEADS // 2, 2, SPAN, HD + 4)
    kept = lax.dynamic_index_in_dim(by_side, core, axis=1, keepdims=False)
    given = lax.dynamic_index_in_dim(by_side, 1 - core, axis=1, keepdims=False)
    taken = lax.ppermute(given, "core", [(0, 1), (1, 0)])
    joined = join_partials(kept, taken)
    parts = lax.all_to_all(joined, "chip", 0, 0, tiled=True)
    part_num = parts[..., :HD].astype(jnp.float32)
    part_max = join_pair(parts[..., HD], parts[..., HD + 1])
    part_sum = join_pair(parts[..., HD + 2], parts[..., HD + 3])

    span_count = span_counts[0]
    query_pos = jnp.arange(SPAN)[:, None]
    key_pos = jnp.arange(SPAN)[None, :]
    span_ok = ((key_pos <= query_pos) & ((key_pos < span_count) | (key_pos == query_pos)))[
        :, None, :
    ]
    own_query = query_own.reshape(SPAN, local_heads, HD)
    own_keys = new_keys.reshape(SPAN, local_heads, HD)
    own_values = new_values.reshape(SPAN, local_heads, HD)
    own_scores = (
        jnp.einsum("qhd,khd->qhk", own_query, own_keys, preferred_element_type=jnp.float32)
        * score_scale
    )
    own_scores = jnp.where(span_ok, own_scores, NEG_LARGE)
    own_max = jnp.max(own_scores, axis=-1)
    own_weights = jnp.where(span_ok, jnp.exp(own_scores - own_max[..., None]), 0.0)
    own_sum = jnp.sum(own_weights, axis=-1)
    own_num = jnp.einsum(
        "qhk,khd->qhd",
        own_weights.astype(jnp.bfloat16),
        own_values,
        preferred_element_type=jnp.float32,
    )
    own_num = own_num.reshape(SPAN, HD)
    own_max = own_max.reshape(SPAN)
    own_sum = own_sum.reshape(SPAN)

    highest = jnp.maximum(jnp.max(part_max, axis=0), own_max)
    part_factor = jnp.exp(part_max - highest)
    own_factor = jnp.exp(own_max - highest)
    numerator = jnp.sum(part_num * part_factor[..., None], axis=0) + own_num * own_factor[:, None]
    totals = jnp.sum(part_sum * part_factor, axis=0) + own_sum * own_factor
    attention = (numerator / totals[:, None]).astype(jnp.bfloat16)

    head_out = jnp.dot(attention, out_weight, preferred_element_type=jnp.float32)
    out_parts = send_rows(head_out.astype(jnp.bfloat16), WIDE, wide_size)
    attn_out = jnp.sum(out_parts.astype(jnp.float32), axis=0)
    normed_mid = rms_scale(attn_out, mlp_gain)
    half_rows = gather_rows(normed_mid, HALF, half_size)
    both = jnp.einsum("gtd,cfd->cgtf", half_rows, chip_gate, preferred_element_type=jnp.float32)
    hidden = (jax.nn.silu(both[0]) * both[1]).astype(jnp.bfloat16)
    ffn_part = jnp.einsum("gtf,fd->gtd", hidden, chip_down, preferred_element_type=jnp.float32)
    ffn_parts = lax.all_to_all(ffn_part.astype(jnp.bfloat16), HALF, 0, 0, tiled=True)
    hidden_out = jnp.sum(ffn_parts.astype(jnp.float32), axis=0).astype(jnp.bfloat16)
    return (hidden_out, attention, new_keys, new_values)


def solution(mesh):
    chips = mesh.shape["wide"] // 2
    split_mesh = jax.sharding.Mesh(
        mesh.devices.reshape(mesh.shape["req"], chips, 2), ("req", "chip", "core")
    )
    return jax.shard_map(
        body,
        mesh=split_mesh,
        in_specs=(
            P(("req",) + WIDE, None),
            P(),
            P(None, None, WIDE),
            P(WIDE, None),
            P(None, None, WIDE),
            P(WIDE, None),
            P(),
            P(None, ("req",) + WIDE, None),
            P(("req",) + WIDE, None),
            P("req", WIDE, None),
            P("req", WIDE, None),
            P("req"),
            P("req", WIDE),
            P("req"),
        ),
        out_specs=(P(("req",) + WIDE, None), P("req", WIDE), P("req", WIDE), P("req", WIDE)),
        check_vma=False,
    )
```

```python
import jax
import jax.numpy as jnp
from jax import lax
from jax.sharding import PartitionSpec as P

D = 7168
HEADS = 32
HD = 224
RANK = 128
SPAN = 128


EPSILON = 1e-05
NEG_LARGE = -1e30
WIDE = ("chip", "core")
HALF = ("req", "chip")


def rms_scale(values, gains):
    widened = values.astype(jnp.float32)
    meansq = jnp.mean(widened * widened, axis=-1, keepdims=True)
    return (widened * lax.rsqrt(meansq + EPSILON) * gains.astype(jnp.float32)).astype(jnp.bfloat16)


def gather_rows(piece, axis, count):
    spread = jnp.broadcast_to(piece[None], (count,) + piece.shape)
    return lax.all_to_all(spread, axis, 0, 0, tiled=True)


def gather_wide(piece, chips):
    own = gather_rows(piece, "chip", chips)[:, None]
    other = lax.ppermute(own, "core", [(0, 1), (1, 0)])
    core = lax.axis_index("core")
    joined = jnp.zeros((chips, 2) + piece.shape, piece.dtype)
    joined = lax.dynamic_update_slice_in_dim(joined, own, core, axis=1)
    joined = lax.dynamic_update_slice_in_dim(joined, other, 1 - core, axis=1)
    return joined.reshape((2 * chips,) + piece.shape)


def send_rows(values, axis, count):
    blocks = values.reshape((count, values.shape[0] // count) + values.shape[1:])
    return lax.all_to_all(blocks, axis, 0, 0, tiled=True)


def split_pair(values):
    high = lax.reduce_precision(values, exponent_bits=8, mantissa_bits=7)
    low = lax.reduce_precision(values - high, exponent_bits=8, mantissa_bits=7)
    return high, low


def join_pair(high, low):
    return high.astype(jnp.float32) + low.astype(jnp.float32)


def join_partials(first, second):
    first_max = join_pair(first[..., HD], first[..., HD + 1])
    second_max = join_pair(second[..., HD], second[..., HD + 1])
    highest = jnp.maximum(first_max, second_max)
    first_factor = jnp.exp(first_max - highest)
    second_factor = jnp.exp(second_max - highest)
    numerator = (
        first[..., :HD].astype(jnp.float32) * first_factor[..., None]
        + second[..., :HD].astype(jnp.float32) * second_factor[..., None]
    )
    totals = join_pair(first[..., HD + 2], first[..., HD + 3]) * first_factor + join_pair(
        second[..., HD + 2], second[..., HD + 3]
    ) * second_factor
    high, low = split_pair(highest)
    shift = jnp.exp(highest - (high + low))
    total_high, total_low = split_pair(totals * shift)
    stats = jnp.stack([high, low, total_high, total_low], axis=-1).astype(jnp.bfloat16)
    return jnp.concatenate([(numerator * shift[..., None]).astype(jnp.bfloat16), stats], axis=-1)


def body(
    tokens,
    attn_gain,
    qkv_weight,
    adapter_down,
    adapter_up,
    out_weight,
    mlp_gain,
    gate_up,
    down_weight,
    key_cache,
    value_cache,
    cache_lengths,
    slot_mask,
    span_counts,
):
    score_scale = HD ** (-0.5)
    wide_size = lax.psum(1, WIDE)
    half_size = lax.psum(1, HALF)
    chips = lax.psum(1, "chip")
    local_width = qkv_weight.shape[2]
    local_heads = local_width // HD
    own_rows = tokens.shape[0]
    wide_index = lax.axis_index(WIDE)
    feature_start = wide_index * local_width

    swap = [(0, 1), (1, 0)]
    chip_gate = jnp.concatenate([gate_up, lax.ppermute(gate_up, "core", swap)], axis=1)
    chip_down = jnp.concatenate([down_weight, lax.ppermute(down_weight, "core", swap)], axis=0)

    normed = rms_scale(tokens, attn_gain)
    shard_rows = gather_wide(normed, chips).reshape(SPAN, D)
    block_len = key_cache.shape[1]
    key_heads = jnp.transpose(key_cache[0].reshape(block_len, HEADS, HD), (1, 0, 2))
    value_heads = jnp.pad(
        jnp.transpose(value_cache[0].reshape(block_len, HEADS, HD), (1, 0, 2)),
        ((0, 0), (0, 0), (0, 4)),
    )
    shard_rows, key_heads, value_heads = lax.optimization_barrier((shard_rows, key_heads, value_heads))
    base_part = lax.optimization_barrier(
        jnp.dot(shard_rows, qkv_weight.reshape(D, 3 * local_width), preferred_element_type=jnp.float32)
    )
    sliced = lax.dynamic_slice_in_dim(shard_rows, feature_start, local_width, 1)
    partial_low = jnp.dot(sliced, adapter_down, preferred_element_type=jnp.float32)
    low_parts = send_rows(partial_low, WIDE, wide_size)
    own_low = jnp.sum(low_parts, axis=0).astype(jnp.bfloat16)
    lowrank = gather_rows(own_low, WIDE, wide_size).reshape(SPAN, 3, RANK)
    adapted = jnp.einsum("tcr,crd->tcd", lowrank, adapter_up, preferred_element_type=jnp.float32)
    projected = (base_part.reshape(SPAN, 3, local_width) + adapted).astype(jnp.bfloat16)
    query_own = projected[:, 0]
    new_keys = projected[:, 1]
    new_values = projected[:, 2]

    query_heads = gather_wide(query_own, chips).reshape(HEADS, SPAN, HD)
    block_start = wide_index * block_len
    length = cache_lengths[0]
    usable = (block_start + jnp.arange(block_len) < length) & (slot_mask[0] == 1)


    def cache_block(unused):
        scores = (
            jnp.einsum("hqd,hkd->hqk", query_heads, key_heads, preferred_element_type=jnp.float32)
            * score_scale
        )
        scores = jnp.where(usable, scores, NEG_LARGE)
        highest = jnp.max(scores, axis=-1)
        high, low = split_pair(highest)
        reference_max = high + low
        weights = jnp.where(usable, jnp.exp(scores - reference_max[..., None]), 0.0)
        totals = jnp.sum(weights, axis=-1)
        numerator = jnp.einsum(
            "hqk,hkd->hqd",
            weights.astype(jnp.bfloat16),
            value_heads,
            preferred_element_type=jnp.float32,
        )
        total_high, total_low = split_pair(totals)
        stats = jnp.stack([high, low, total_high, total_low], axis=-1).astype(jnp.bfloat16)
        return lax.dynamic_update_slice(numerator.astype(jnp.bfloat16), stats, (0, 0, HD))

    def skipped(unused):
        stats = jnp.zeros((HEADS, SPAN, 4), jnp.bfloat16).at[..., 0].set(NEG_LARGE)
        return jnp.concatenate([jnp.zeros((HEADS, SPAN, HD), jnp.bfloat16), stats], axis=-1)

    packed = lax.cond(block_start < length, cache_block, skipped, 0)
    core = lax.axis_index("core")
    by_side = packed.reshape(HEADS // 2, 2, SPAN, HD + 4)
    kept = lax.dynamic_index_in_dim(by_side, core, axis=1, keepdims=False)
    given = lax.dynamic_index_in_dim(by_side, 1 - core, axis=1, keepdims=False)
    taken = lax.ppermute(given, "core", [(0, 1), (1, 0)])
    joined = join_partials(kept, taken)
    parts = lax.all_to_all(joined, "chip", 0, 0, tiled=True)
    part_num = parts[..., :HD].astype(jnp.float32)
    part_max = join_pair(parts[..., HD], parts[..., HD + 1])
    part_sum = join_pair(parts[..., HD + 2], parts[..., HD + 3])

    span_count = span_counts[0]
    query_pos = jnp.arange(SPAN)[:, None]
    key_pos = jnp.arange(SPAN)[None, :]
    span_ok = ((key_pos <= query_pos) & ((key_pos < span_count) | (key_pos == query_pos)))[
        :, None, :
    ]
    own_query = query_own.reshape(SPAN, local_heads, HD)
    own_keys = new_keys.reshape(SPAN, local_heads, HD)
    own_values = new_values.reshape(SPAN, local_heads, HD)
    own_scores = (
        jnp.einsum("qhd,khd->qhk", own_query, own_keys, preferred_element_type=jnp.float32)
        * score_scale
    )
    own_scores = jnp.where(span_ok, own_scores, NEG_LARGE)
    own_max = jnp.max(own_scores, axis=-1)
    own_weights = jnp.where(span_ok, jnp.exp(own_scores - own_max[..., None]), 0.0)
    own_sum = jnp.sum(own_weights, axis=-1)
    own_num = jnp.einsum(
        "qhk,khd->qhd",
        own_weights.astype(jnp.bfloat16),
        own_values,
        preferred_element_type=jnp.float32,
    )
    own_num = own_num.reshape(SPAN, HD)
    own_max = own_max.reshape(SPAN)
    own_sum = own_sum.reshape(SPAN)

    highest = jnp.maximum(jnp.max(part_max, axis=0), own_max)
    part_factor = jnp.exp(part_max - highest)
    own_factor = jnp.exp(own_max - highest)
    numerator = jnp.sum(part_num * part_factor[..., None], axis=0) + own_num * own_factor[:, None]
    totals = jnp.sum(part_sum * part_factor, axis=0) + own_sum * own_factor
    attention = (numerator / totals[:, None]).astype(jnp.bfloat16)

    head_out = jnp.dot(attention, out_weight, preferred_element_type=jnp.float32)
    out_sides = head_out.reshape(chips, 2, own_rows, -1)
    out_kept = lax.dynamic_index_in_dim(out_sides, core, axis=1, keepdims=False)
    out_given = lax.dynamic_index_in_dim(out_sides, 1 - core, axis=1, keepdims=False)
    out_taken = lax.ppermute(out_given.astype(jnp.bfloat16), "core", [(0, 1), (1, 0)])
    out_chip = (out_kept + out_taken.astype(jnp.float32)).astype(jnp.bfloat16)
    out_parts = lax.all_to_all(out_chip, "chip", 0, 0, tiled=True)
    attn_out = jnp.sum(out_parts.astype(jnp.float32), axis=0)
    normed_mid = rms_scale(attn_out, mlp_gain)
    half_rows = gather_rows(normed_mid, HALF, half_size)
    both = jnp.einsum("gtd,cfd->cgtf", half_rows, chip_gate, preferred_element_type=jnp.float32)
    hidden = (jax.nn.silu(both[0]) * both[1]).astype(jnp.bfloat16)
    ffn_part = jnp.einsum("gtf,fd->gtd", hidden, chip_down, preferred_element_type=jnp.float32)
    ffn_parts = lax.all_to_all(ffn_part.astype(jnp.bfloat16), HALF, 0, 0, tiled=True)
    hidden_out = jnp.sum(ffn_parts.astype(jnp.float32), axis=0).astype(jnp.bfloat16)
    return (hidden_out, attention, new_keys, new_values)


def solution(mesh):
    chips = mesh.shape["wide"] // 2
    split_mesh = jax.sharding.Mesh(
        mesh.devices.reshape(mesh.shape["req"], chips, 2), ("req", "chip", "core")
    )
    return jax.shard_map(
        body,
        mesh=split_mesh,
        in_specs=(
            P(("req",) + WIDE, None),
            P(),
            P(None, None, WIDE),
            P(WIDE, None),
            P(None, None, WIDE),
            P(WIDE, None),
            P(),
            P(None, ("req",) + WIDE, None),
            P(("req",) + WIDE, None),
            P("req", WIDE, None),
            P("req", WIDE, None),
            P("req"),
            P("req", WIDE),
            P("req"),
        ),
        out_specs=(P(("req",) + WIDE, None), P("req", WIDE), P("req", WIDE), P("req", WIDE)),
        check_vma=False,
    )
```

```python
import jax
import jax.numpy as jnp
from jax import lax
from jax.sharding import PartitionSpec as P

D = 7168
HEADS = 32
HD = 224
RANK = 128
SPAN = 128


EPSILON = 1e-05
NEG_LARGE = -1e30
WIDE = ("chip", "core")
HALF = ("req", "chip")


def rms_scale(values, gains):
    widened = values.astype(jnp.float32)
    meansq = jnp.mean(widened * widened, axis=-1, keepdims=True)
    return (widened * lax.rsqrt(meansq + EPSILON) * gains.astype(jnp.float32)).astype(jnp.bfloat16)


def gather_rows(piece, axis, count):
    spread = jnp.broadcast_to(piece[None], (count,) + piece.shape)
    return lax.all_to_all(spread, axis, 0, 0, tiled=True)


def gather_wide(piece, chips):
    own = gather_rows(piece, "chip", chips)[:, None]
    other = lax.ppermute(own, "core", [(0, 1), (1, 0)])
    core = lax.axis_index("core")
    joined = jnp.zeros((chips, 2) + piece.shape, piece.dtype)
    joined = lax.dynamic_update_slice_in_dim(joined, own, core, axis=1)
    joined = lax.dynamic_update_slice_in_dim(joined, other, 1 - core, axis=1)
    return joined.reshape((2 * chips,) + piece.shape)


def send_rows(values, axis, count):
    blocks = values.reshape((count, values.shape[0] // count) + values.shape[1:])
    return lax.all_to_all(blocks, axis, 0, 0, tiled=True)


def split_pair(values):
    high = lax.reduce_precision(values, exponent_bits=8, mantissa_bits=7)
    low = lax.reduce_precision(values - high, exponent_bits=8, mantissa_bits=7)
    return high, low


def join_pair(high, low):
    return high.astype(jnp.float32) + low.astype(jnp.float32)


def join_partials(first, second):
    first_max = join_pair(first[..., HD], first[..., HD + 1])
    second_max = join_pair(second[..., HD], second[..., HD + 1])
    highest = jnp.maximum(first_max, second_max)
    first_factor = jnp.exp(first_max - highest)
    second_factor = jnp.exp(second_max - highest)
    numerator = (
        first[..., :HD].astype(jnp.float32) * first_factor[..., None]
        + second[..., :HD].astype(jnp.float32) * second_factor[..., None]
    )
    totals = join_pair(first[..., HD + 2], first[..., HD + 3]) * first_factor + join_pair(
        second[..., HD + 2], second[..., HD + 3]
    ) * second_factor
    high, low = split_pair(highest)
    shift = jnp.exp(highest - (high + low))
    total_high, total_low = split_pair(totals * shift)
    stats = jnp.stack([high, low, total_high, total_low], axis=-1).astype(jnp.bfloat16)
    return jnp.concatenate([(numerator * shift[..., None]).astype(jnp.bfloat16), stats], axis=-1)


def body(
    tokens,
    attn_gain,
    qkv_weight,
    adapter_down,
    adapter_up,
    out_weight,
    mlp_gain,
    gate_up,
    down_weight,
    key_cache,
    value_cache,
    cache_lengths,
    slot_mask,
    span_counts,
):
    score_scale = HD ** (-0.5)
    wide_size = lax.psum(1, WIDE)
    half_size = lax.psum(1, HALF)
    chips = lax.psum(1, "chip")
    local_width = qkv_weight.shape[2]
    local_heads = local_width // HD
    own_rows = tokens.shape[0]
    wide_index = lax.axis_index(WIDE)
    feature_start = wide_index * local_width

    swap = [(0, 1), (1, 0)]
    sibling_gate = lax.ppermute(gate_up, "core", swap)
    sibling_down = lax.ppermute(down_weight, "core", swap)

    normed = rms_scale(tokens, attn_gain)
    shard_rows = gather_wide(normed, chips).reshape(SPAN, D)
    block_len = key_cache.shape[1]
    key_heads = jnp.transpose(key_cache[0].reshape(block_len, HEADS, HD), (1, 0, 2))
    value_heads = jnp.pad(
        jnp.transpose(value_cache[0].reshape(block_len, HEADS, HD), (1, 0, 2)),
        ((0, 0), (0, 0), (0, 4)),
    )
    shard_rows, key_heads, value_heads = lax.optimization_barrier((shard_rows, key_heads, value_heads))
    base_part = lax.optimization_barrier(
        jnp.dot(shard_rows, qkv_weight.reshape(D, 3 * local_width), preferred_element_type=jnp.float32)
    )
    sliced = lax.dynamic_slice_in_dim(shard_rows, feature_start, local_width, 1)
    partial_low = jnp.dot(sliced, adapter_down, preferred_element_type=jnp.float32)
    low_parts = send_rows(partial_low, WIDE, wide_size)
    own_low = jnp.sum(low_parts, axis=0).astype(jnp.bfloat16)
    lowrank = gather_rows(own_low, WIDE, wide_size).reshape(SPAN, 3, RANK)
    adapted = jnp.einsum("tcr,crd->tcd", lowrank, adapter_up, preferred_element_type=jnp.float32)
    projected = (base_part.reshape(SPAN, 3, local_width) + adapted).astype(jnp.bfloat16)
    query_own = projected[:, 0]
    new_keys = projected[:, 1]
    new_values = projected[:, 2]

    query_heads = gather_wide(query_own, chips).reshape(HEADS, SPAN, HD)
    block_start = wide_index * block_len
    length = cache_lengths[0]
    usable = (block_start + jnp.arange(block_len) < length) & (slot_mask[0] == 1)


    def cache_block(unused):
        scores = (
            jnp.einsum("hqd,hkd->hqk", query_heads, key_heads, preferred_element_type=jnp.float32)
            * score_scale
        )
        scores = jnp.where(usable, scores, NEG_LARGE)
        highest = jnp.max(scores, axis=-1)
        high, low = split_pair(highest)
        reference_max = high + low
        weights = jnp.where(usable, jnp.exp(scores - reference_max[..., None]), 0.0)
        totals = jnp.sum(weights, axis=-1)
        numerator = jnp.einsum(
            "hqk,hkd->hqd",
            weights.astype(jnp.bfloat16),
            value_heads,
            preferred_element_type=jnp.float32,
        )
        total_high, total_low = split_pair(totals)
        stats = jnp.stack([high, low, total_high, total_low], axis=-1).astype(jnp.bfloat16)
        return lax.dynamic_update_slice(numerator.astype(jnp.bfloat16), stats, (0, 0, HD))

    def skipped(unused):
        stats = jnp.zeros((HEADS, SPAN, 4), jnp.bfloat16).at[..., 0].set(NEG_LARGE)
        return jnp.concatenate([jnp.zeros((HEADS, SPAN, HD), jnp.bfloat16), stats], axis=-1)

    packed = lax.cond(block_start < length, cache_block, skipped, 0)
    core = lax.axis_index("core")
    by_side = packed.reshape(HEADS // 2, 2, SPAN, HD + 4)
    kept = lax.dynamic_index_in_dim(by_side, core, axis=1, keepdims=False)
    given = lax.dynamic_index_in_dim(by_side, 1 - core, axis=1, keepdims=False)
    taken = lax.ppermute(given, "core", [(0, 1), (1, 0)])
    joined = join_partials(kept, taken)
    parts = lax.all_to_all(joined, "chip", 0, 0, tiled=True)
    part_num = parts[..., :HD].astype(jnp.float32)
    part_max = join_pair(parts[..., HD], parts[..., HD + 1])
    part_sum = join_pair(parts[..., HD + 2], parts[..., HD + 3])

    span_count = span_counts[0]
    query_pos = jnp.arange(SPAN)[:, None]
    key_pos = jnp.arange(SPAN)[None, :]
    span_ok = ((key_pos <= query_pos) & ((key_pos < span_count) | (key_pos == query_pos)))[
        :, None, :
    ]
    own_query = query_own.reshape(SPAN, local_heads, HD)
    own_keys = new_keys.reshape(SPAN, local_heads, HD)
    own_values = new_values.reshape(SPAN, local_heads, HD)
    own_scores = (
        jnp.einsum("qhd,khd->qhk", own_query, own_keys, preferred_element_type=jnp.float32)
        * score_scale
    )
    own_scores = jnp.where(span_ok, own_scores, NEG_LARGE)
    own_max = jnp.max(own_scores, axis=-1)
    own_weights = jnp.where(span_ok, jnp.exp(own_scores - own_max[..., None]), 0.0)
    own_sum = jnp.sum(own_weights, axis=-1)
    own_num = jnp.einsum(
        "qhk,khd->qhd",
        own_weights.astype(jnp.bfloat16),
        own_values,
        preferred_element_type=jnp.float32,
    )
    own_num = own_num.reshape(SPAN, HD)
    own_max = own_max.reshape(SPAN)
    own_sum = own_sum.reshape(SPAN)

    highest = jnp.maximum(jnp.max(part_max, axis=0), own_max)
    part_factor = jnp.exp(part_max - highest)
    own_factor = jnp.exp(own_max - highest)
    numerator = jnp.sum(part_num * part_factor[..., None], axis=0) + own_num * own_factor[:, None]
    totals = jnp.sum(part_sum * part_factor, axis=0) + own_sum * own_factor
    attention = (numerator / totals[:, None]).astype(jnp.bfloat16)

    head_out = jnp.dot(attention, out_weight, preferred_element_type=jnp.float32)
    out_sides = head_out.reshape(chips, 2, own_rows, -1)
    out_kept = lax.dynamic_index_in_dim(out_sides, core, axis=1, keepdims=False)
    out_given = lax.dynamic_index_in_dim(out_sides, 1 - core, axis=1, keepdims=False)
    out_taken = lax.ppermute(out_given.astype(jnp.bfloat16), "core", [(0, 1), (1, 0)])
    out_chip = (out_kept + out_taken.astype(jnp.float32)).astype(jnp.bfloat16)
    out_parts = lax.all_to_all(out_chip, "chip", 0, 0, tiled=True)
    attn_out = jnp.sum(out_parts.astype(jnp.float32), axis=0)
    normed_mid = rms_scale(attn_out, mlp_gain)
    half_rows = gather_rows(normed_mid, HALF, half_size)
    ffn_part = None
    for gate_rows, down_rows in ((gate_up, down_weight), (sibling_gate, sibling_down)):
        both = jnp.einsum("gtd,cfd->cgtf", half_rows, gate_rows, preferred_element_type=jnp.float32)
        hidden = (jax.nn.silu(both[0]) * both[1]).astype(jnp.bfloat16)
        term = jnp.einsum("gtf,fd->gtd", hidden, down_rows, preferred_element_type=jnp.float32)
        ffn_part = term if ffn_part is None else ffn_part + term
    ffn_parts = lax.all_to_all(ffn_part.astype(jnp.bfloat16), HALF, 0, 0, tiled=True)
    hidden_out = jnp.sum(ffn_parts.astype(jnp.float32), axis=0).astype(jnp.bfloat16)
    return (hidden_out, attention, new_keys, new_values)


def solution(mesh):
    chips = mesh.shape["wide"] // 2
    split_mesh = jax.sharding.Mesh(
        mesh.devices.reshape(mesh.shape["req"], chips, 2), ("req", "chip", "core")
    )
    return jax.shard_map(
        body,
        mesh=split_mesh,
        in_specs=(
            P(("req",) + WIDE, None),
            P(),
            P(None, None, WIDE),
            P(WIDE, None),
            P(None, None, WIDE),
            P(WIDE, None),
            P(),
            P(None, ("req",) + WIDE, None),
            P(("req",) + WIDE, None),
            P("req", WIDE, None),
            P("req", WIDE, None),
            P("req"),
            P("req", WIDE),
            P("req"),
        ),
        out_specs=(P(("req",) + WIDE, None), P("req", WIDE), P("req", WIDE), P("req", WIDE)),
        check_vma=False,
    )
```
